32 devices in a mesh: dp: 16 (over z, x, core), group: 2 (over y).
Axes of the slice: x: 2, y: 2, z: 4, core: 2. Of those that a mesh axis runs over, the one named last changes fastest.
Arguments:
- atom_feats: bfloat16 [256, 32, 512], P(('dp', 'group')), may hold values from -6 to 6
- coords: float32 [256, 3, 32], P(('dp', 'group')), may hold values from -6 to 6
- atom_counts: int32 [256], P(('dp', 'group')), may hold values from 8 to 32
- positives: int32 [256], P(('dp', 'group')), may hold values from 0 to 255, each once
- z2: bfloat16 [256, 128], P(('dp', 'group')), may hold values from -6 to 6
- w_qkv: bfloat16 [512, 1536], replicated, may hold values from -0.25 to 0.25
- w_out: bfloat16 [512, 512], replicated, may hold values from -0.25 to 0.25
- proj: bfloat16 [512, 128], replicated, may hold values from -0.25 to 0.25
- bias_weight: float32 [128, 64], replicated, may hold values from -2 to 36
- ln_gain: float32 [512], replicated, may hold values from 0.5 to 1.5
Outputs:
- loss: float32 [], replicated
- grad_z2: float32 [256, 128], P(('dp', 'group'))
- grad_w_qkv: float32 [512, 1536], replicated
- grad_w_out: float32 [512, 512], replicated
- grad_proj: float32 [512, 128], replicated
- grad_bias_weight: float32 [128, 64], replicated
- grad_ln_gain: float32 [512], replicated
The draws below stay inside these ranges and needn't reach their ends.
Inputs may be any that keep to these rules, and one draw needn't show every extreme that they name: positives is a permutation of the 256 molecules.
All inputs are finite; a program needn't handle non-finite values.
Results may differ from the reference program's by a relative error of at most 0.014.
Values may be sent and summed in bfloat16 or wider, within the bound.
No kernel may reach another device: no remote copies, remote signals or barrier semaphores. Data moves between devices by JAX's collectives and lax.ppermute only.
A program may use at most 128 MiB of HBM per device.

```python
import jax
import jax.numpy as jnp
from jax import lax

D = 512
HEADS = 64
P_SIZE = 128
KERNELS = 128
ATOMS = 32
MOL_DEV = 8
BATCH = 256


def draw_bias_weight(key, part):
    rough = jnp.clip(0.3 * jax.random.normal(jax.random.fold_in(key, 11), (KERNELS, HEADS), jnp.float32), -2.0, 2.0)
    return rough


def plant(result, own_key, smallest, high):
    dims = result.shape
    spot = [jax.random.randint(jax.random.fold_in(own_key, axis), (), 0, dims[axis]) for axis in range(len(dims))]
    result = result.at[tuple(spot)].set(smallest)
    longest = dims.index(max(dims))
    spot[longest] = (spot[longest] + 1) % dims[longest]
    return result.at[tuple(spot)].set(high)


def block_scale(key, extent, shards, least, largest):
    def one(position, parts):
        heights = jax.random.uniform(jax.random.fold_in(jax.random.fold_in(key, 6), position), (parts,), jnp.float32, least / len(shards), largest / len(shards))
        return jnp.repeat(jnp.exp(heights), extent[position] // parts).reshape((-1,) + (1,) * (len(extent) - position - 1))

    factor_of = one(*shards[0])
    for cut in shards[1:]:
        factor_of = factor_of * one(*cut)
    return factor_of


def centred(rng, dims, scale, bound, cuts=(), dtype=jnp.bfloat16):
    values = jax.random.normal(rng, dims, jnp.float32) * scale
    if len(cuts) > 0:
        values = block_scale(rng, dims, cuts, -0.22, 0.18) * values
    return jnp.clip(values, min=-bound, max=bound).astype(dtype)


def setup_inputs(seed: int = 0) -> dict:
    key_list = jax.random.split(jax.random.key(seed), 11)
    return {
        "atom_feats": centred(key_list[0], (BATCH, ATOMS, D), 1.0, 6.0, ((0, 32),)),
        "coords": centred(key_list[1], (BATCH, 3, ATOMS), 1.5, 6.0, ((0, 32),), jnp.float32),
        "atom_counts": plant(jax.random.randint(key_list[2], (BATCH,), ATOMS // 4, ATOMS + 1), jax.random.fold_in(key_list[2], 1), ATOMS // 4, ATOMS).astype(jnp.int32),
        "positives": jax.random.permutation(key_list[3], BATCH).astype(jnp.int32),
        "z2": centred(key_list[4], (BATCH, P_SIZE), 1.0, 6.0, ((0, 32),)),
        "w_qkv": centred(key_list[5], (D, 3 * D), D ** -0.5, 0.25),
        "w_out": centred(key_list[6], (D, D), D ** -0.5, 0.25),
        "proj": centred(key_list[7], (D, P_SIZE), D ** -0.5, 0.25),
        "bias_weight": draw_bias_weight(jax.random.fold_in(key_list[10], 71), 0),
        "ln_gain": jnp.clip(1.0 + 0.1 * jax.random.normal(key_list[9], (D,), jnp.float32), 0.5, 1.5),
    }


def encode(weights_all, feats, coords, counts):
    w_qkv, w_out, proj, bias_weight, ln_gain = weights_all
    mol_count, atom_count, model_width = feats.shape
    kernels = bias_weight.shape[0]
    head_count = bias_weight.shape[1]
    head_dim = model_width // head_count
    inputs = feats.astype(jnp.float32)
    center = lax.optimization_barrier(jnp.mean(inputs, axis=-1, keepdims=True))
    spread = lax.optimization_barrier(jnp.mean((inputs - center) ** 2, axis=-1, keepdims=True))
    normed = ((inputs - center) * lax.rsqrt(spread + 1e-05) * ln_gain).astype(jnp.bfloat16)
    projected = jnp.dot(normed.reshape(mol_count * atom_count, model_width), w_qkv, preferred_element_type=jnp.float32).astype(jnp.bfloat16)
    projected = projected.reshape(mol_count, atom_count, 3, head_count, head_dim)
    query_heads = projected[:, :, 0]
    key_heads = projected[:, :, 1]
    value_heads = projected[:, :, 2]
    offsets = coords[:, :, :, None] - coords[:, :, None, :]
    distance = jnp.sqrt(lax.optimization_barrier(jnp.sum(offsets * offsets, axis=1)) + 0.25)
    centers = jnp.arange(kernels).astype(jnp.float32) * (12.0 / kernels)
    kernel_basis = jnp.exp(-((distance[..., None] - centers) / 0.5) ** 2)
    pair_bias = jnp.einsum('mijk,kh->mhij', kernel_basis, bias_weight, precision=lax.Precision.HIGHEST)
    scores = jnp.einsum('mihd,mjhd->mhij', query_heads, key_heads, preferred_element_type=jnp.float32) * head_dim ** (-0.5) + pair_bias
    is_valid = jnp.arange(atom_count)[None, :] < counts[:, None]
    scores = jnp.where(is_valid[:, None, None, :], scores, -1e+30)
    highest = lax.optimization_barrier(jnp.max(scores, axis=-1, keepdims=True))
    expo = jnp.exp(scores - highest)
    attn_weights = (expo / lax.optimization_barrier(jnp.sum(expo, axis=-1, keepdims=True))).astype(jnp.bfloat16)
    context = jnp.einsum('mhij,mjhd->mihd', attn_weights, value_heads, preferred_element_type=jnp.float32).astype(jnp.bfloat16)
    hidden = inputs + jnp.dot(context.reshape(mol_count * atom_count, model_width), w_out, preferred_element_type=jnp.float32).reshape(mol_count, atom_count, model_width)
    pooled = lax.optimization_barrier(jnp.sum(jnp.where(is_valid[..., None], hidden, 0.0), axis=1))
    return jnp.dot(pooled.astype(jnp.bfloat16), proj, preferred_element_type=jnp.float32)

def unit_rows(values):
    inverse = lax.rsqrt(lax.optimization_barrier(jnp.mean(values * values, axis=1, keepdims=True)) + 1e-06) * values.shape[1] ** (-0.5)
    return (values * inverse, inverse)

def unit_backward(values, inverse, grad):
    along = lax.optimization_barrier(jnp.sum(values * grad, axis=1, keepdims=True))
    return inverse * (grad - values * along * (inverse * inverse))

def reference(atom_feats, coords, atom_counts, positives, z2, w_qkv, w_out, proj, bias_weight, ln_gain):
    weights_all = (w_qkv, w_out, proj, bias_weight, ln_gain)
    blocks = BATCH // MOL_DEV
    feat_blocks = atom_feats.reshape(blocks, MOL_DEV, ATOMS, D)
    coord_blocks = coords.reshape(blocks, MOL_DEV, 3, ATOMS)
    count_blocks = atom_counts.reshape(blocks, MOL_DEV)

    def forward_block(entries):
        return encode(weights_all, entries[0], entries[1], entries[2])
    z3 = lax.map(forward_block, (feat_blocks, coord_blocks, count_blocks)).reshape(BATCH, P_SIZE)
    unit, inverse = unit_rows(z3)
    z3_half = unit.astype(jnp.bfloat16)
    row_blocks = z3_half.reshape(blocks, MOL_DEV, P_SIZE)
    target_blocks = positives.reshape(blocks, MOL_DEV)
    columns = jnp.arange(BATCH).astype(jnp.int32)

    def first_pass(col_total, entries):
        logits = jnp.dot(entries[0], z2.T, preferred_element_type=jnp.float32)
        expo = jnp.exp(logits)
        row_lse = jnp.log(lax.optimization_barrier(jnp.sum(expo, axis=1)))
        is_positive = entries[1][:, None] == columns[None, :]
        positive_score = lax.optimization_barrier(jnp.sum(jnp.where(is_positive, logits, 0.0), axis=1))
        return (col_total + lax.optimization_barrier(jnp.sum(expo, axis=0)), (row_lse, jnp.sum(0.5 * row_lse - positive_score)))
    col_total, (lse_blocks, row_terms) = lax.scan(first_pass, jnp.zeros((BATCH,), jnp.float32), (row_blocks, target_blocks))
    col_lse = jnp.log(col_total)
    loss = (jnp.sum(row_terms) + 0.5 * jnp.sum(col_lse)) / BATCH

    def second_pass(grad_cols, entries):
        logits = jnp.dot(entries[0], z2.T, preferred_element_type=jnp.float32)
        is_positive = entries[1][:, None] == columns[None, :]
        slope = (0.5 * jnp.exp(logits - entries[2][:, None]) + 0.5 * jnp.exp(logits - col_lse[None, :]) - is_positive.astype(jnp.float32)).astype(jnp.bfloat16)
        grad_rows = jnp.dot(slope, z2, preferred_element_type=jnp.float32)
        grad_cols = grad_cols + lax.dot_general(slope, entries[0], (((0,), (0,)), ((), ())), preferred_element_type=jnp.float32)
        return (grad_cols, grad_rows)
    grad_z2, unit_grads = lax.scan(second_pass, jnp.zeros((BATCH, P_SIZE), jnp.float32), (row_blocks, target_blocks, lse_blocks))
    grad_z3 = unit_backward(z3, inverse, unit_grads.reshape(BATCH, P_SIZE))
    grad_blocks = grad_z3.reshape(blocks, MOL_DEV, P_SIZE)

    def accumulate(running, entries):

        def local_encode(params_in):
            return encode(params_in, entries[0], entries[1], entries[2])
        unused, pullback = jax.vjp(local_encode, weights_all)
        pieces = pullback(entries[3])[0]
        return (tuple((a + b.astype(jnp.float32) for a, b in zip(running, pieces))), None)
    start_sums = tuple((jnp.zeros(w.shape, jnp.float32) for w in weights_all))
    sums, unused = lax.scan(accumulate, start_sums, (feat_blocks, coord_blocks, count_blocks, grad_blocks))
    return (loss, grad_z2, sums[0], sums[1], sums[2], sums[3], sums[4])
```

```python
import math

import jax
import jax.numpy as jnp
from jax import lax
from jax.sharding import PartitionSpec as P


def pair_distance(coords):
    offsets = coords[:, :, :, None] - coords[:, :, None, :]
    return jnp.sqrt(jnp.sum(offsets * offsets, axis=1) + 0.25)


def kernel_values(distance, kernels):
    centers = jnp.arange(kernels).astype(jnp.float32) * (12.0 / kernels)
    return jnp.exp(-(((distance[..., None] - centers) / 0.5) ** 2))


def group_split(values, width):
    return values.reshape((values.shape[0] // width, width) + values.shape[1:])


def bias_forward(distance, bias_weight):
    mol_count = distance.shape[0]
    width = math.gcd(mol_count, 8)

    def one_group(group_distance):
        basis = kernel_values(group_distance, bias_weight.shape[0])
        return jnp.einsum("mijk,kh->mhij", basis, bias_weight, precision=lax.Precision.HIGHEST)

    biased = lax.map(one_group, group_split(distance, width))
    return biased.reshape((mol_count,) + biased.shape[2:])


def bias_backward(distance, bias_slope, kernels):
    width = math.gcd(distance.shape[0], 8)

    def add_group(running, pieces):
        basis = kernel_values(pieces[0], kernels)
        return (
            running
            + jnp.einsum("mijk,mhij->kh", basis, pieces[1], precision=lax.Precision.HIGHEST),
            None,
        )

    start_sum = jnp.zeros((kernels, bias_slope.shape[1]), jnp.float32)
    summed, unused = lax.scan(
        add_group, start_sum, (group_split(distance, width), group_split(bias_slope, width))
    )
    return summed


def encode_core(params_in, pair_bias, feats, counts):
    w_qkv, w_out, proj, ln_gain = params_in
    mol_count, atom_count, model_width = feats.shape
    head_count = pair_bias.shape[1]
    head_dim = model_width // head_count
    inputs = feats.astype(jnp.float32)
    center = jnp.mean(inputs, axis=-1, keepdims=True)
    spread = jnp.mean((inputs - center) ** 2, axis=-1, keepdims=True)
    normed = ((inputs - center) * lax.rsqrt(spread + 1e-05) * ln_gain).astype(jnp.bfloat16)
    projected = jnp.dot(
        normed.reshape(mol_count * atom_count, model_width),
        w_qkv,
        preferred_element_type=jnp.float32,
    ).astype(jnp.bfloat16)
    projected = projected.reshape(mol_count, atom_count, 3, head_count, head_dim)
    query_heads = projected[:, :, 0]
    key_heads = projected[:, :, 1]
    value_heads = projected[:, :, 2]
    scores = (
        jnp.einsum("mihd,mjhd->mhij", query_heads, key_heads, preferred_element_type=jnp.float32)
        * head_dim ** (-0.5)
        + pair_bias
    )
    is_valid = jnp.arange(atom_count)[None, :] < counts[:, None]
    scores = jnp.where(is_valid[:, None, None, :], scores, -1e30)
    highest = jnp.max(scores, axis=-1, keepdims=True)
    expo = jnp.exp(scores - highest)
    attn_weights = (expo / jnp.sum(expo, axis=-1, keepdims=True)).astype(jnp.bfloat16)
    context = jnp.einsum(
        "mhij,mjhd->mihd", attn_weights, value_heads, preferred_element_type=jnp.float32
    ).astype(jnp.bfloat16)
    hidden = inputs + jnp.dot(
        context.reshape(mol_count * atom_count, model_width),
        w_out,
        preferred_element_type=jnp.float32,
    ).reshape(mol_count, atom_count, model_width)
    pooled = jnp.sum(jnp.where(is_valid[..., None], hidden, 0.0), axis=1)
    return jnp.dot(pooled.astype(jnp.bfloat16), proj, preferred_element_type=jnp.float32)


def unit_rows(values):
    inverse = lax.rsqrt(jnp.mean(values * values, axis=1, keepdims=True) + 1e-06) * values.shape[
        1
    ] ** (-0.5)
    return (values * inverse, inverse)


def unit_backward(values, inverse, grad):
    along = jnp.sum(values * grad, axis=1, keepdims=True)
    return inverse * (grad - values * along * (inverse * inverse))


def on_device(
    atom_feats, coords, atom_counts, positives, z2, w_qkv, w_out, proj, bias_weight, ln_gain
):
    distance = pair_distance(coords)
    pair_bias = bias_forward(distance, bias_weight)

    def local_encode(params_in, bias_in):
        return encode_core(params_in, bias_in, atom_feats, atom_counts)

    z3, pullback = jax.vjp(local_encode, (w_qkv, w_out, proj, ln_gain), pair_bias)
    unit, inverse = unit_rows(z3)
    z3_half = unit.astype(jnp.bfloat16)
    own_rows = z3.shape[0]
    width = z3.shape[1]
    packed = jnp.concatenate(
        [
            z3_half.astype(jnp.float32),
            z2.astype(jnp.float32),
            positives.astype(jnp.float32)[:, None],
        ],
        axis=1,
    )
    gathered = lax.all_gather(packed, ("dp", "group"), axis=0, tiled=True)
    z3_all = gathered[:, :width].astype(jnp.bfloat16)
    z2_all = gathered[:, width : 2 * width].astype(jnp.bfloat16)
    pos_all = gathered[:, 2 * width].astype(jnp.int32)
    batch_rows = z2_all.shape[0]
    logits = jnp.dot(z3_all, z2_all.T, preferred_element_type=jnp.float32)
    expo = jnp.exp(logits)
    row_lse = jnp.log(jnp.sum(expo, axis=1))
    col_lse = jnp.log(jnp.sum(expo, axis=0))
    columns = jnp.arange(batch_rows)
    is_positive = pos_all[:, None] == columns[None, :]
    positive_score = jnp.sum(jnp.where(is_positive, logits, 0.0), axis=1)
    loss = (jnp.sum(0.5 * row_lse - positive_score) + 0.5 * jnp.sum(col_lse)) / batch_rows
    slope = (
        0.5 * jnp.exp(logits - row_lse[:, None])
        + 0.5 * jnp.exp(logits - col_lse[None, :])
        - is_positive.astype(jnp.float32)
    ).astype(jnp.bfloat16)
    block = lax.axis_index("dp") * lax.axis_size("group") + lax.axis_index("group")
    first = block * own_rows
    grad_cols = lax.dot_general(
        slope, z3_all, (((0,), (0,)), ((), ())), preferred_element_type=jnp.float32
    )
    grad_z2 = lax.dynamic_slice_in_dim(grad_cols, first, own_rows, axis=0)
    grad_rows = jnp.dot(slope, z2_all, preferred_element_type=jnp.float32)
    grad_unit = lax.dynamic_slice_in_dim(grad_rows, first, own_rows, axis=0)
    grad_z3 = unit_backward(z3, inverse, grad_unit)
    pieces, bias_slope = pullback(grad_z3)
    grad_bias = bias_backward(distance, bias_slope, bias_weight.shape[0])
    kernels = bias_weight.shape[0]
    heads = bias_weight.shape[1]
    lanes = proj.shape[1]
    small = jnp.concatenate(
        [
            pieces[2],
            grad_bias.reshape(-1, lanes).astype(jnp.bfloat16),
            pieces[3].reshape(-1, lanes).astype(jnp.bfloat16),
        ],
        axis=0,
    )
    totals = lax.psum((pieces[0], pieces[1], small), ("dp", "group"))
    totals = [t.astype(jnp.float32) for t in totals]
    proj_rows = proj.shape[0]
    bias_rows = kernels * heads // lanes
    grad_proj = totals[2][:proj_rows]
    grad_bias_all = totals[2][proj_rows : proj_rows + bias_rows].reshape(kernels, heads)
    grad_gain = totals[2][proj_rows + bias_rows :].reshape(-1)
    return (loss, grad_z2, totals[0], totals[1], grad_proj, grad_bias_all, grad_gain)


def solution(mesh):
    return jax.shard_map(
        on_device,
        mesh=mesh,
        in_specs=(
            P(("dp", "group"), None, None),
            P(("dp", "group"), None, None),
            P(("dp", "group")),
            P(("dp", "group")),
            P(("dp", "group"), None),
            P(),
            P(),
            P(),
            P(),
            P(),
        ),
        out_specs=(P(), P(("dp", "group"), None), P(), P(), P(), P(), P()),
        check_vma=False,
    )
```

```python
import math

import jax
import jax.numpy as jnp
from jax import lax
from jax.sharding import PartitionSpec as P


def pair_distance(coords):
    offsets = coords[:, :, :, None] - coords[:, :, None, :]
    return jnp.sqrt(jnp.sum(offsets * offsets, axis=1) + 0.25)


def kernel_values(distance, kernels):
    centers = jnp.arange(kernels).astype(jnp.float32) * (12.0 / kernels)
    return jnp.exp(-(((distance[..., None] - centers) / 0.5) ** 2))


def group_split(values, width):
    return values.reshape((values.shape[0] // width, width) + values.shape[1:])


def bias_forward(distance, bias_weight):
    mol_count = distance.shape[0]
    width = math.gcd(mol_count, 8)

    def one_group(group_distance):
        basis = kernel_values(group_distance, bias_weight.shape[0])
        return jnp.einsum("mijk,kh->mhij", basis, bias_weight, precision=lax.Precision.HIGHEST)

    biased = lax.map(one_group, group_split(distance, width))
    return biased.reshape((mol_count,) + biased.shape[2:])


def bias_backward(distance, bias_slope, kernels):
    width = math.gcd(distance.shape[0], 8)

    def add_group(running, pieces):
        basis = kernel_values(pieces[0], kernels)
        return (
            running
            + jnp.einsum("mijk,mhij->kh", basis, pieces[1], precision=lax.Precision.HIGHEST),
            None,
        )

    start_sum = jnp.zeros((kernels, bias_slope.shape[1]), jnp.float32)
    summed, unused = lax.scan(
        add_group, start_sum, (group_split(distance, width), group_split(bias_slope, width))
    )
    return summed


def encode_core(params_in, pair_bias, feats, counts):
    w_qkv, w_out, proj, ln_gain = params_in
    mol_count, atom_count, model_width = feats.shape
    head_count = pair_bias.shape[1]
    head_dim = model_width // head_count
    inputs = feats.astype(jnp.float32)
    center = jnp.mean(inputs, axis=-1, keepdims=True)
    spread = jnp.mean((inputs - center) ** 2, axis=-1, keepdims=True)
    normed = ((inputs - center) * lax.rsqrt(spread + 1e-05) * ln_gain).astype(jnp.bfloat16)
    projected = jnp.dot(
        normed.reshape(mol_count * atom_count, model_width),
        w_qkv,
        preferred_element_type=jnp.float32,
    ).astype(jnp.bfloat16)
    projected = projected.reshape(mol_count, atom_count, 3, head_count, head_dim)
    query_heads = projected[:, :, 0]
    key_heads = projected[:, :, 1]
    value_heads = projected[:, :, 2]
    scores = (
        jnp.einsum("mihd,mjhd->mhij", query_heads, key_heads, preferred_element_type=jnp.float32)
        * head_dim ** (-0.5)
        + pair_bias
    )
    is_valid = jnp.arange(atom_count)[None, :] < counts[:, None]
    scores = jnp.where(is_valid[:, None, None, :], scores, -1e30)
    highest = jnp.max(scores, axis=-1, keepdims=True)
    expo = jnp.exp(scores - highest)
    attn_weights = (expo / jnp.sum(expo, axis=-1, keepdims=True)).astype(jnp.bfloat16)
    context = jnp.einsum(
        "mhij,mjhd->mihd", attn_weights, value_heads, preferred_element_type=jnp.float32
    ).astype(jnp.bfloat16)
    hidden = inputs + jnp.dot(
        context.reshape(mol_count * atom_count, model_width),
        w_out,
        preferred_element_type=jnp.float32,
    ).reshape(mol_count, atom_count, model_width)
    pooled = jnp.sum(jnp.where(is_valid[..., None], hidden, 0.0), axis=1)
    return jnp.dot(pooled.astype(jnp.bfloat16), proj, preferred_element_type=jnp.float32)


def unit_rows(values):
    inverse = lax.rsqrt(jnp.mean(values * values, axis=1, keepdims=True) + 1e-06) * values.shape[
        1
    ] ** (-0.5)
    return (values * inverse, inverse)


def unit_backward(values, inverse, grad):
    along = jnp.sum(values * grad, axis=1, keepdims=True)
    return inverse * (grad - values * along * (inverse * inverse))


def flat_index():
    return lax.axis_index("dp") * lax.axis_size("group") + lax.axis_index("group")


def device_count():
    return lax.axis_size("dp") * lax.axis_size("group")


def step_bits(count):
    steps = count.bit_length() - 1
    assert 1 << steps == count
    order = [1, 0] + list(range(2, steps)) if steps >= 2 else list(range(steps))
    return order


def swap_with(value, bit, count):
    pairs = [(i, i ^ (1 << bit)) for i in range(count)]
    return lax.ppermute(value, ("dp", "group"), pairs)


def gather_rows(value):
    count = device_count()
    index = flat_index()
    current = value
    for bit in range(count.bit_length() - 1):
        other = swap_with(current, bit, count)
        low = (index >> bit) % 2 == 0
        current = jnp.where(
            low, jnp.concatenate([current, other]), jnp.concatenate([other, current])
        )
    return current


def sum_rows(values):
    count = device_count()
    index = flat_index()
    order = step_bits(count)
    current = [v.astype(jnp.float32) for v in values]
    for bit in order:
        side = (index >> bit) % 2
        kept, sent = [], []
        for v in current:
            half = v.shape[0] // 2
            kept.append(lax.dynamic_slice_in_dim(v, side * half, half, axis=0))
            sent.append(lax.dynamic_slice_in_dim(v, (1 - side) * half, half, axis=0))
        came = swap_with(tuple(s.astype(jnp.bfloat16) for s in sent), bit, count)
        current = [k + c.astype(jnp.float32) for k, c in zip(kept, came)]
    current = [v.astype(jnp.bfloat16) for v in current]
    for bit in reversed(order):
        low = (index >> bit) % 2 == 0
        came = swap_with(tuple(current), bit, count)
        current = [
            jnp.where(low, jnp.concatenate([v, c]), jnp.concatenate([c, v]))
            for v, c in zip(current, came)
        ]
    return [v.astype(jnp.float32) for v in current]


def on_device(
    atom_feats, coords, atom_counts, positives, z2, w_qkv, w_out, proj, bias_weight, ln_gain
):
    distance = pair_distance(coords)
    pair_bias = bias_forward(distance, bias_weight)

    def local_encode(params_in, bias_in):
        return encode_core(params_in, bias_in, atom_feats, atom_counts)

    z3, pullback = jax.vjp(local_encode, (w_qkv, w_out, proj, ln_gain), pair_bias)
    unit, inverse = unit_rows(z3)
    z3_half = unit.astype(jnp.bfloat16)
    own_rows = z3.shape[0]
    width = z3.shape[1]
    scale = 128
    packed = jnp.concatenate(
        [
            z3_half,
            z2,
            (positives // scale).astype(jnp.bfloat16)[:, None],
            (positives % scale).astype(jnp.bfloat16)[:, None],
        ],
        axis=1,
    )
    gathered = gather_rows(packed)
    z3_all = gathered[:, :width]
    z2_all = gathered[:, width : 2 * width]
    pos_all = gathered[:, 2 * width].astype(jnp.int32) * scale + gathered[:, 2 * width + 1].astype(
        jnp.int32
    )
    batch_rows = z2_all.shape[0]
    logits = jnp.dot(z3_all, z2_all.T, preferred_element_type=jnp.float32)
    expo = jnp.exp(logits)
    row_lse = jnp.log(jnp.sum(expo, axis=1))
    col_lse = jnp.log(jnp.sum(expo, axis=0))
    columns = jnp.arange(batch_rows)
    is_positive = pos_all[:, None] == columns[None, :]
    positive_score = jnp.sum(jnp.where(is_positive, logits, 0.0), axis=1)
    loss = (jnp.sum(0.5 * row_lse - positive_score) + 0.5 * jnp.sum(col_lse)) / batch_rows
    slope = (
        0.5 * jnp.exp(logits - row_lse[:, None])
        + 0.5 * jnp.exp(logits - col_lse[None, :])
        - is_positive.astype(jnp.float32)
    ).astype(jnp.bfloat16)
    block = flat_index()
    first = block * own_rows
    grad_cols = lax.dot_general(
        slope, z3_all, (((0,), (0,)), ((), ())), preferred_element_type=jnp.float32
    )
    grad_z2 = lax.dynamic_slice_in_dim(grad_cols, first, own_rows, axis=0)
    grad_rows = jnp.dot(slope, z2_all, preferred_element_type=jnp.float32)
    grad_unit = lax.dynamic_slice_in_dim(grad_rows, first, own_rows, axis=0)
    grad_z3 = unit_backward(z3, inverse, grad_unit)
    pieces, bias_slope = pullback(grad_z3)
    grad_bias = bias_backward(distance, bias_slope, bias_weight.shape[0])
    kernels = bias_weight.shape[0]
    heads = bias_weight.shape[1]
    lanes = proj.shape[1]
    small = jnp.concatenate(
        [
            pieces[2],
            grad_bias.reshape(-1, lanes).astype(jnp.bfloat16),
            pieces[3].reshape(-1, lanes).astype(jnp.bfloat16),
        ],
        axis=0,
    )
    small_rows = small.shape[0]
    unit = 8 * device_count()
    padded = -(-small_rows // unit) * unit
    small = jnp.pad(small, ((0, padded - small_rows), (0, 0)))
    totals = sum_rows((pieces[0], pieces[1], small))
    proj_rows = proj.shape[0]
    bias_rows = kernels * heads // lanes
    grad_proj = totals[2][:proj_rows]
    grad_bias_all = totals[2][proj_rows : proj_rows + bias_rows].reshape(kernels, heads)
    gain_rows = ln_gain.shape[0] // lanes
    grad_gain = totals[2][proj_rows + bias_rows : proj_rows + bias_rows + gain_rows].reshape(-1)
    return (loss, grad_z2, totals[0], totals[1], grad_proj, grad_bias_all, grad_gain)


def solution(mesh):
    return jax.shard_map(
        on_device,
        mesh=mesh,
        in_specs=(
            P(("dp", "group"), None, None),
            P(("dp", "group"), None, None),
            P(("dp", "group")),
            P(("dp", "group")),
            P(("dp", "group"), None),
            P(),
            P(),
            P(),
            P(),
            P(),
        ),
        out_specs=(P(), P(("dp", "group"), None), P(), P(), P(), P(), P()),
        check_vma=False,
    )
```

```python
import math

import jax
import jax.numpy as jnp
from jax import lax
from jax.sharding import PartitionSpec as P


def pair_distance(coords):
    offsets = coords[:, :, :, None] - coords[:, :, None, :]
    return jnp.sqrt(jnp.sum(offsets * offsets, axis=1) + 0.25)


def kernel_values(distance, kernels):
    centers = jnp.arange(kernels).astype(jnp.float32) * (12.0 / kernels)
    return jnp.exp(-(((distance[..., None] - centers) / 0.5) ** 2))


def group_split(values, width):
    return values.reshape((values.shape[0] // width, width) + values.shape[1:])


def bias_forward(distance, bias_weight):
    mol_count = distance.shape[0]
    width = math.gcd(mol_count, 8)

    def one_group(group_distance):
        basis = kernel_values(group_distance, bias_weight.shape[0])
        return jnp.einsum("mijk,kh->mhij", basis, bias_weight, precision=lax.Precision.HIGHEST)

    biased = lax.map(one_group, group_split(distance, width))
    return biased.reshape((mol_count,) + biased.shape[2:])


def bias_backward(distance, bias_slope, kernels):
    width = math.gcd(distance.shape[0], 8)

    def add_group(running, pieces):
        basis = kernel_values(pieces[0], kernels)
        return (
            running
            + jnp.einsum("mijk,mhij->kh", basis, pieces[1], precision=lax.Precision.HIGHEST),
            None,
        )

    start_sum = jnp.zeros((kernels, bias_slope.shape[1]), jnp.float32)
    summed, unused = lax.scan(
        add_group, start_sum, (group_split(distance, width), group_split(bias_slope, width))
    )
    return summed


def encode_core(params_in, pair_bias, feats, counts):
    w_qkv, w_out, proj, ln_gain = params_in
    mol_count, atom_count, model_width = feats.shape
    head_count = pair_bias.shape[1]
    head_dim = model_width // head_count
    inputs = feats.astype(jnp.float32)
    center = jnp.mean(inputs, axis=-1, keepdims=True)
    spread = jnp.mean((inputs - center) ** 2, axis=-1, keepdims=True)
    normed = ((inputs - center) * lax.rsqrt(spread + 1e-05) * ln_gain).astype(jnp.bfloat16)
    projected = jnp.dot(
        normed.reshape(mol_count * atom_count, model_width),
        w_qkv,
        preferred_element_type=jnp.float32,
    ).astype(jnp.bfloat16)
    projected = projected.reshape(mol_count, atom_count, 3, head_count, head_dim)
    query_heads = projected[:, :, 0]
    key_heads = projected[:, :, 1]
    value_heads = projected[:, :, 2]
    scores = (
        jnp.einsum("mihd,mjhd->mhij", query_heads, key_heads, preferred_element_type=jnp.float32)
        * head_dim ** (-0.5)
        + pair_bias
    )
    is_valid = jnp.arange(atom_count)[None, :] < counts[:, None]
    scores = jnp.where(is_valid[:, None, None, :], scores, -1e30)
    highest = jnp.max(scores, axis=-1, keepdims=True)
    expo = jnp.exp(scores - highest)
    attn_weights = (expo / jnp.sum(expo, axis=-1, keepdims=True)).astype(jnp.bfloat16)
    context = jnp.einsum(
        "mhij,mjhd->mihd", attn_weights, value_heads, preferred_element_type=jnp.float32
    ).astype(jnp.bfloat16)
    hidden = inputs + jnp.dot(
        context.reshape(mol_count * atom_count, model_width),
        w_out,
        preferred_element_type=jnp.float32,
    ).reshape(mol_count, atom_count, model_width)
    pooled = jnp.sum(jnp.where(is_valid[..., None], hidden, 0.0), axis=1)
    return jnp.dot(pooled.astype(jnp.bfloat16), proj, preferred_element_type=jnp.float32)


def unit_rows(values):
    inverse = lax.rsqrt(jnp.mean(values * values, axis=1, keepdims=True) + 1e-06) * values.shape[
        1
    ] ** (-0.5)
    return (values * inverse, inverse)


def unit_backward(values, inverse, grad):
    along = jnp.sum(values * grad, axis=1, keepdims=True)
    return inverse * (grad - values * along * (inverse * inverse))


def flat_index():
    return lax.axis_index("dp") * lax.axis_size("group") + lax.axis_index("group")


def device_count():
    return lax.axis_size("dp") * lax.axis_size("group")


def step_bits(count):
    steps = count.bit_length() - 1
    assert 1 << steps == count
    order = [1, 0] + list(range(2, steps)) if steps >= 2 else list(range(steps))
    return order


def swap_with(value, bit, count):
    pairs = [(i, i ^ (1 << bit)) for i in range(count)]
    return lax.ppermute(value, ("dp", "group"), pairs)


def gather_rows(value):
    count = device_count()
    index = flat_index()
    current = value
    for bit in range(count.bit_length() - 1):
        other = swap_with(current, bit, count)
        low = (index >> bit) % 2 == 0
        current = jnp.where(
            low, jnp.concatenate([current, other]), jnp.concatenate([other, current])
        )
    return current


def sum_rows(values):
    count = device_count()
    index = flat_index()
    order = step_bits(count)
    current = [v.astype(jnp.float32) for v in values]
    for bit in order:
        side = (index >> bit) % 2
        kept, sent = [], []
        for v in current:
            half = v.shape[0] // 2
            kept.append(lax.dynamic_slice_in_dim(v, side * half, half, axis=0))
            sent.append(lax.dynamic_slice_in_dim(v, (1 - side) * half, half, axis=0))
        came = swap_with(tuple(s.astype(jnp.bfloat16) for s in sent), bit, count)
        current = [k + c.astype(jnp.float32) for k, c in zip(kept, came)]
    current = [v.astype(jnp.bfloat16) for v in current]
    for bit in reversed(order):
        low = (index >> bit) % 2 == 0
        came = swap_with(tuple(current), bit, count)
        current = [
            jnp.where(low, jnp.concatenate([v, c]), jnp.concatenate([c, v]))
            for v, c in zip(current, came)
        ]
    return [v.astype(jnp.float32) for v in current]


def on_device(
    atom_feats, coords, atom_counts, positives, z2, w_qkv, w_out, proj, bias_weight, ln_gain
):
    distance = pair_distance(coords)
    pair_bias = bias_forward(distance, bias_weight)

    def local_encode(params_in, bias_in):
        return encode_core(params_in, bias_in, atom_feats, atom_counts)

    z3, pullback = jax.vjp(local_encode, (w_qkv, w_out, proj, ln_gain), pair_bias)
    unit, inverse = unit_rows(z3)
    z3_half = unit.astype(jnp.bfloat16)
    own_rows = z3.shape[0]
    width = z3.shape[1]
    scale = 128
    packed = jnp.concatenate(
        [
            z3_half,
            z2,
            (positives // scale).astype(jnp.bfloat16)[:, None],
            (positives % scale).astype(jnp.bfloat16)[:, None],
        ],
        axis=1,
    )
    gathered = gather_rows(packed)
    z3_all = gathered[:, :width]
    z2_all = gathered[:, width : 2 * width]
    pos_all = gathered[:, 2 * width].astype(jnp.int32) * scale + gathered[:, 2 * width + 1].astype(
        jnp.int32
    )
    batch_rows = z2_all.shape[0]
    logits = jnp.dot(z3_all, z2_all.T, preferred_element_type=jnp.float32)
    expo = jnp.exp(logits)
    row_lse = jnp.log(jnp.sum(expo, axis=1))
    col_lse = jnp.log(jnp.sum(expo, axis=0))
    columns = jnp.arange(batch_rows)
    is_positive = pos_all[:, None] == columns[None, :]
    positive_score = jnp.sum(jnp.where(is_positive, logits, 0.0), axis=1)
    loss = (jnp.sum(0.5 * row_lse - positive_score) + 0.5 * jnp.sum(col_lse)) / batch_rows
    slope = (
        0.5 * jnp.exp(logits - row_lse[:, None])
        + 0.5 * jnp.exp(logits - col_lse[None, :])
        - is_positive.astype(jnp.float32)
    ).astype(jnp.bfloat16)
    block = flat_index()
    first = block * own_rows
    grad_cols = lax.dot_general(
        slope, z3_all, (((0,), (0,)), ((), ())), preferred_element_type=jnp.float32
    )
    grad_z2 = lax.dynamic_slice_in_dim(grad_cols, first, own_rows, axis=0)
    grad_rows = jnp.dot(slope, z2_all, preferred_element_type=jnp.float32)
    grad_unit = lax.dynamic_slice_in_dim(grad_rows, first, own_rows, axis=0)
    grad_z3 = unit_backward(z3, inverse, grad_unit)
    pieces, bias_slope = pullback(grad_z3)
    grad_bias = bias_backward(distance, bias_slope, bias_weight.shape[0])
    big = jnp.concatenate([pieces[0], pieces[1]], axis=1)
    span = big.shape[1]
    small = jnp.concatenate(
        [
            pieces[2].reshape(-1),
            grad_bias.reshape(-1).astype(jnp.bfloat16),
            pieces[3].reshape(-1).astype(jnp.bfloat16),
        ]
    )
    small_size = small.shape[0]
    small_rows = -(-small_size // span)
    small = jnp.pad(small, (0, small_rows * span - small_size)).reshape(small_rows, span)
    count = device_count()
    rows = big.shape[0] + small_rows
    padded = -(-rows // count) * count
    joined = jnp.concatenate(
        [big, small, jnp.zeros((padded - rows, span), jnp.bfloat16)], axis=0
    )
    (total,) = sum_rows((joined,))
    qkv_cols = w_qkv.shape[1]
    weight_rows = w_qkv.shape[0]
    grad_qkv = total[:weight_rows, :qkv_cols]
    grad_out = total[:weight_rows, qkv_cols:]
    tail = total[weight_rows : weight_rows + small_rows].reshape(-1)
    proj_size = proj.size
    bias_size = bias_weight.size
    grad_proj = tail[:proj_size].reshape(proj.shape)
    grad_bias_all = tail[proj_size : proj_size + bias_size].reshape(bias_weight.shape)
    grad_gain = tail[proj_size + bias_size : proj_size + bias_size + ln_gain.size]
    return (loss, grad_z2, grad_qkv, grad_out, grad_proj, grad_bias_all, grad_gain)


def solution(mesh):
    return jax.shard_map(
        on_device,
        mesh=mesh,
        in_specs=(
            P(("dp", "group"), None, None),
            P(("dp", "group"), None, None),
            P(("dp", "group")),
            P(("dp", "group")),
            P(("dp", "group"), None),
            P(),
            P(),
            P(),
            P(),
            P(),
        ),
        out_specs=(P(), P(("dp", "group"), None), P(), P(), P(), P(), P()),
        check_vma=False,
    )
```

```python
import math

import jax
import jax.numpy as jnp
from jax import lax
from jax.sharding import PartitionSpec as P


def pair_distance(coords):
    offsets = coords[:, :, :, None] - coords[:, :, None, :]
    return jnp.sqrt(jnp.sum(offsets * offsets, axis=1) + 0.25)


def kernel_values(distance, kernels):
    centers = jnp.arange(kernels).astype(jnp.float32) * (12.0 / kernels)
    return jnp.exp(-(((distance[..., None] - centers) / 0.5) ** 2))


def group_split(values, width):
    return values.reshape((values.shape[0] // width, width) + values.shape[1:])


def bias_forward(distance, bias_weight):
    mol_count = distance.shape[0]
    width = math.gcd(mol_count, 8)

    def one_group(group_distance):
        basis = kernel_values(group_distance, bias_weight.shape[0])
        return jnp.einsum("mijk,kh->mhij", basis, bias_weight, precision=lax.Precision.HIGHEST)

    biased = lax.map(one_group, group_split(distance, width))
    return biased.reshape((mol_count,) + biased.shape[2:])


def bias_backward(distance, bias_slope, kernels):
    width = math.gcd(distance.shape[0], 8)

    def add_group(running, pieces):
        basis = kernel_values(pieces[0], kernels)
        return (
            running
            + jnp.einsum("mijk,mhij->kh", basis, pieces[1], precision=lax.Precision.HIGHEST),
            None,
        )

    start_sum = jnp.zeros((kernels, bias_slope.shape[1]), jnp.float32)
    summed, unused = lax.scan(
        add_group, start_sum, (group_split(distance, width), group_split(bias_slope, width))
    )
    return summed


def encode_core(params_in, pair_bias, feats, counts):
    w_qkv, w_out, proj, ln_gain = params_in
    mol_count, atom_count, model_width = feats.shape
    head_count = pair_bias.shape[1]
    head_dim = model_width // head_count
    inputs = feats.astype(jnp.float32)
    center = jnp.mean(inputs, axis=-1, keepdims=True)
    spread = jnp.mean((inputs - center) ** 2, axis=-1, keepdims=True)
    normed = ((inputs - center) * lax.rsqrt(spread + 1e-05) * ln_gain).astype(jnp.bfloat16)
    projected = jnp.dot(
        normed.reshape(mol_count * atom_count, model_width),
        w_qkv,
        preferred_element_type=jnp.float32,
    ).astype(jnp.bfloat16)
    projected = projected.reshape(mol_count, atom_count, 3, head_count, head_dim)
    query_heads = projected[:, :, 0]
    key_heads = projected[:, :, 1]
    value_heads = projected[:, :, 2]
    scores = (
        jnp.einsum("mihd,mjhd->mhij", query_heads, key_heads, preferred_element_type=jnp.float32)
        * head_dim ** (-0.5)
        + pair_bias
    )
    is_valid = jnp.arange(atom_count)[None, :] < counts[:, None]
    scores = jnp.where(is_valid[:, None, None, :], scores, -1e30)
    highest = jnp.max(scores, axis=-1, keepdims=True)
    expo = jnp.exp(scores - highest)
    attn_weights = (expo / jnp.sum(expo, axis=-1, keepdims=True)).astype(jnp.bfloat16)
    context = jnp.einsum(
        "mhij,mjhd->mihd", attn_weights, value_heads, preferred_element_type=jnp.float32
    ).astype(jnp.bfloat16)
    hidden = inputs + jnp.dot(
        context.reshape(mol_count * atom_count, model_width),
        w_out,
        preferred_element_type=jnp.float32,
    ).reshape(mol_count, atom_count, model_width)
    pooled = jnp.sum(jnp.where(is_valid[..., None], hidden, 0.0), axis=1)
    return jnp.dot(pooled.astype(jnp.bfloat16), proj, preferred_element_type=jnp.float32)


def unit_rows(values):
    inverse = lax.rsqrt(jnp.mean(values * values, axis=1, keepdims=True) + 1e-06) * values.shape[
        1
    ] ** (-0.5)
    return (values * inverse, inverse)


def unit_backward(values, inverse, grad):
    along = jnp.sum(values * grad, axis=1, keepdims=True)
    return inverse * (grad - values * along * (inverse * inverse))


def flat_index():
    return lax.axis_index("dp") * lax.axis_size("group") + lax.axis_index("group")


def device_count():
    return lax.axis_size("dp") * lax.axis_size("group")


def step_bits(count, part=0, parts=1):
    steps = count.bit_length() - 1
    assert 1 << steps == count
    if steps < 2:
        return list(range(steps))
    outer = [0] + list(range(2, steps))
    turn = (part * len(outer)) // parts
    return [1] + outer[turn:] + outer[:turn]


def swap_with(value, bit, count):
    pairs = [(i, i ^ (1 << bit)) for i in range(count)]
    return lax.ppermute(value, ("dp", "group"), pairs)


def gather_rows(value):
    count = device_count()
    index = flat_index()
    current = value
    for bit in range(count.bit_length() - 1):
        other = swap_with(current, bit, count)
        low = (index >> bit) % 2 == 0
        current = jnp.where(
            low, jnp.concatenate([current, other]), jnp.concatenate([other, current])
        )
    return current


def sum_rows(values, parts=1):
    count = device_count()
    index = flat_index()
    orders = [step_bits(count, p, parts) for p in range(parts)]
    current = []
    for v in values:
        share = v.shape[0] // parts
        current += [v[p * share : (p + 1) * share].astype(jnp.float32) for p in range(parts)]
    order_of = [orders[i % parts] for i in range(len(current))]
    for step in range(len(orders[0])):
        sent_all, kept_all = [], []
        for v, order in zip(current, order_of):
            side = (index >> order[step]) % 2
            half = v.shape[0] // 2
            kept_all.append(lax.dynamic_slice_in_dim(v, side * half, half, axis=0))
            sent = lax.dynamic_slice_in_dim(v, (1 - side) * half, half, axis=0)
            sent_all.append(swap_with(sent.astype(jnp.bfloat16), order[step], count))
        current = [k + c.astype(jnp.float32) for k, c in zip(kept_all, sent_all)]
    current = [v.astype(jnp.bfloat16) for v in current]
    for step in reversed(range(len(orders[0]))):
        joined = []
        for v, order in zip(current, order_of):
            low = (index >> order[step]) % 2 == 0
            c = swap_with(v, order[step], count)
            joined.append(jnp.where(low, jnp.concatenate([v, c]), jnp.concatenate([c, v])))
        current = joined
    merged = []
    for i in range(len(values)):
        merged.append(jnp.concatenate(current[i * parts : (i + 1) * parts]).astype(jnp.float32))
    return merged


def on_device(
    atom_feats, coords, atom_counts, positives, z2, w_qkv, w_out, proj, bias_weight, ln_gain
):
    distance = pair_distance(coords)
    pair_bias = bias_forward(distance, bias_weight)

    def local_encode(params_in, bias_in):
        return encode_core(params_in, bias_in, atom_feats, atom_counts)

    z3, pullback = jax.vjp(local_encode, (w_qkv, w_out, proj, ln_gain), pair_bias)
    unit, inverse = unit_rows(z3)
    z3_half = unit.astype(jnp.bfloat16)
    own_rows = z3.shape[0]
    width = z3.shape[1]
    scale = 128
    packed = jnp.concatenate(
        [
            z3_half,
            z2,
            (positives // scale).astype(jnp.bfloat16)[:, None],
            (positives % scale).astype(jnp.bfloat16)[:, None],
        ],
        axis=1,
    )
    gathered = gather_rows(packed)
    z3_all = gathered[:, :width]
    z2_all = gathered[:, width : 2 * width]
    pos_all = gathered[:, 2 * width].astype(jnp.int32) * scale + gathered[:, 2 * width + 1].astype(
        jnp.int32
    )
    batch_rows = z2_all.shape[0]
    logits = jnp.dot(z3_all, z2_all.T, preferred_element_type=jnp.float32)
    expo = jnp.exp(logits)
    row_lse = jnp.log(jnp.sum(expo, axis=1))
    col_lse = jnp.log(jnp.sum(expo, axis=0))
    columns = jnp.arange(batch_rows)
    is_positive = pos_all[:, None] == columns[None, :]
    positive_score = jnp.sum(jnp.where(is_positive, logits, 0.0), axis=1)
    loss = (jnp.sum(0.5 * row_lse - positive_score) + 0.5 * jnp.sum(col_lse)) / batch_rows
    slope = (
        0.5 * jnp.exp(logits - row_lse[:, None])
        + 0.5 * jnp.exp(logits - col_lse[None, :])
        - is_positive.astype(jnp.float32)
    ).astype(jnp.bfloat16)
    block = flat_index()
    first = block * own_rows
    grad_cols = lax.dot_general(
        slope, z3_all, (((0,), (0,)), ((), ())), preferred_element_type=jnp.float32
    )
    grad_z2 = lax.dynamic_slice_in_dim(grad_cols, first, own_rows, axis=0)
    grad_rows = jnp.dot(slope, z2_all, preferred_element_type=jnp.float32)
    grad_unit = lax.dynamic_slice_in_dim(grad_rows, first, own_rows, axis=0)
    grad_z3 = unit_backward(z3, inverse, grad_unit)
    pieces, bias_slope = pullback(grad_z3)
    grad_bias = bias_backward(distance, bias_slope, bias_weight.shape[0])
    big = jnp.concatenate([pieces[0], pieces[1]], axis=1)
    span = big.shape[1]
    small = jnp.concatenate(
        [
            pieces[2].reshape(-1),
            grad_bias.reshape(-1).astype(jnp.bfloat16),
            pieces[3].reshape(-1).astype(jnp.bfloat16),
        ]
    )
    small_size = small.shape[0]
    small_rows = -(-small_size // span)
    small = jnp.pad(small, (0, small_rows * span - small_size)).reshape(small_rows, span)
    count = device_count()
    rows = big.shape[0] + small_rows
    parts = 2
    padded = -(-rows // (count * parts)) * (count * parts)
    joined = jnp.concatenate(
        [big, small, jnp.zeros((padded - rows, span), jnp.bfloat16)], axis=0
    )
    (total,) = sum_rows((joined,), parts)
    qkv_cols = w_qkv.shape[1]
    weight_rows = w_qkv.shape[0]
    grad_qkv = total[:weight_rows, :qkv_cols]
    grad_out = total[:weight_rows, qkv_cols:]
    tail = total[weight_rows : weight_rows + small_rows].reshape(-1)
    proj_size = proj.size
    bias_size = bias_weight.size
    grad_proj = tail[:proj_size].reshape(proj.shape)
    grad_bias_all = tail[proj_size : proj_size + bias_size].reshape(bias_weight.shape)
    grad_gain = tail[proj_size + bias_size : proj_size + bias_size + ln_gain.size]
    return (loss, grad_z2, grad_qkv, grad_out, grad_proj, grad_bias_all, grad_gain)


def solution(mesh):
    return jax.shard_map(
        on_device,
        mesh=mesh,
        in_specs=(
            P(("dp", "group"), None, None),
            P(("dp", "group"), None, None),
            P(("dp", "group")),
            P(("dp", "group")),
            P(("dp", "group"), None),
            P(),
            P(),
            P(),
            P(),
            P(),
        ),
        out_specs=(P(), P(("dp", "group"), None), P(), P(), P(), P(), P()),
        check_vma=False,
    )
```

```python
import math

import jax
import jax.numpy as jnp
from jax import lax
from jax.sharding import PartitionSpec as P


def pair_distance(coords):
    offsets = coords[:, :, :, None] - coords[:, :, None, :]
    return jnp.sqrt(jnp.sum(offsets * offsets, axis=1) + 0.25)


def kernel_values(distance, kernels):
    centers = jnp.arange(kernels).astype(jnp.float32) * (12.0 / kernels)
    return jnp.exp(-(((distance[..., None] - centers) / 0.5) ** 2))


def group_split(values, width):
    return values.reshape((values.shape[0] // width, width) + values.shape[1:])


def bias_forward(distance, bias_weight):
    basis = kernel_values(distance, bias_weight.shape[0])
    return jnp.einsum("mijk,kh->mhij", basis, bias_weight, precision=lax.Precision.HIGHEST)


def bias_backward(distance, bias_slope, kernels):
    basis = kernel_values(distance, kernels)
    return jnp.einsum("mijk,mhij->kh", basis, bias_slope, precision=lax.Precision.HIGHEST)


def encode_core(params_in, pair_bias, feats, counts):
    w_qkv, w_out, proj, ln_gain = params_in
    mol_count, atom_count, model_width = feats.shape
    head_count = pair_bias.shape[1]
    head_dim = model_width // head_count
    inputs = feats.astype(jnp.float32)
    center = jnp.mean(inputs, axis=-1, keepdims=True)
    spread = jnp.mean((inputs - center) ** 2, axis=-1, keepdims=True)
    normed = ((inputs - center) * lax.rsqrt(spread + 1e-05) * ln_gain).astype(jnp.bfloat16)
    split_weight = w_qkv.reshape(model_width, 3, head_count, head_dim)
    projected = jnp.einsum(
        "mia,achd->cmhid", normed, split_weight, preferred_element_type=jnp.float32
    ).astype(jnp.bfloat16)
    query_heads = projected[0]
    key_heads = projected[1]
    value_heads = projected[2]
    scores = (
        jnp.einsum("mhid,mhjd->mhij", query_heads, key_heads, preferred_element_type=jnp.float32)
        * head_dim ** (-0.5)
        + pair_bias
    )
    is_valid = jnp.arange(atom_count)[None, :] < counts[:, None]
    scores = jnp.where(is_valid[:, None, None, :], scores, -1e30)
    highest = jnp.max(scores, axis=-1, keepdims=True)
    expo = jnp.exp(scores - highest)
    attn_weights = (expo / jnp.sum(expo, axis=-1, keepdims=True)).astype(jnp.bfloat16)
    context = jnp.einsum(
        "mhij,mhjd->mihd", attn_weights, value_heads, preferred_element_type=jnp.float32
    ).astype(jnp.bfloat16)
    hidden = inputs + jnp.dot(
        context.reshape(mol_count * atom_count, model_width),
        w_out,
        preferred_element_type=jnp.float32,
    ).reshape(mol_count, atom_count, model_width)
    pooled = jnp.sum(jnp.where(is_valid[..., None], hidden, 0.0), axis=1)
    return jnp.dot(pooled.astype(jnp.bfloat16), proj, preferred_element_type=jnp.float32)


def unit_rows(values):
    inverse = lax.rsqrt(jnp.mean(values * values, axis=1, keepdims=True) + 1e-06) * values.shape[
        1
    ] ** (-0.5)
    return (values * inverse, inverse)


def unit_backward(values, inverse, grad):
    along = jnp.sum(values * grad, axis=1, keepdims=True)
    return inverse * (grad - values * along * (inverse * inverse))


def flat_index():
    return lax.axis_index("dp") * lax.axis_size("group") + lax.axis_index("group")


def device_count():
    return lax.axis_size("dp") * lax.axis_size("group")


def step_bits(count, part=0, parts=1):
    steps = count.bit_length() - 1
    assert 1 << steps == count
    if steps < 2:
        return list(range(steps))
    outer = [0] + list(range(2, steps))
    turn = (part * len(outer)) // parts
    return [1] + outer[turn:] + outer[:turn]


def swap_with(value, bit, count):
    pairs = [(i, i ^ (1 << bit)) for i in range(count)]
    return lax.ppermute(value, ("dp", "group"), pairs)


def gather_rows(value):
    count = device_count()
    index = flat_index()
    current = value
    for bit in range(count.bit_length() - 1):
        other = swap_with(current, bit, count)
        low = (index >> bit) % 2 == 0
        current = jnp.where(
            low, jnp.concatenate([current, other]), jnp.concatenate([other, current])
        )
    return current


def sum_rows(values, parts=1):
    count = device_count()
    index = flat_index()
    orders = [step_bits(count, p, parts) for p in range(parts)]
    current = []
    for v in values:
        share = v.shape[0] // parts
        current += [v[p * share : (p + 1) * share].astype(jnp.float32) for p in range(parts)]
    order_of = [orders[i % parts] for i in range(len(current))]
    for step in range(len(orders[0])):
        sent_all, kept_all = [], []
        for v, order in zip(current, order_of):
            side = (index >> order[step]) % 2
            half = v.shape[0] // 2
            kept_all.append(lax.dynamic_slice_in_dim(v, side * half, half, axis=0))
            sent = lax.dynamic_slice_in_dim(v, (1 - side) * half, half, axis=0)
            sent_all.append(swap_with(sent.astype(jnp.bfloat16), order[step], count))
        current = [k + c.astype(jnp.float32) for k, c in zip(kept_all, sent_all)]
    current = [v.astype(jnp.bfloat16) for v in current]
    for step in reversed(range(len(orders[0]))):
        joined = []
        for v, order in zip(current, order_of):
            low = (index >> order[step]) % 2 == 0
            c = swap_with(v, order[step], count)
            joined.append(jnp.where(low, jnp.concatenate([v, c]), jnp.concatenate([c, v])))
        current = joined
    merged = []
    for i in range(len(values)):
        merged.append(jnp.concatenate(current[i * parts : (i + 1) * parts]).astype(jnp.float32))
    return merged


def on_device(
    atom_feats, coords, atom_counts, positives, z2, w_qkv, w_out, proj, bias_weight, ln_gain
):
    distance = pair_distance(coords)
    pair_bias = bias_forward(distance, bias_weight)

    def local_encode(params_in, bias_in):
        return encode_core(params_in, bias_in, atom_feats, atom_counts)

    z3, pullback = jax.vjp(local_encode, (w_qkv, w_out, proj, ln_gain), pair_bias)
    unit, inverse = unit_rows(z3)
    z3_half = unit.astype(jnp.bfloat16)
    own_rows = z3.shape[0]
    width = z3.shape[1]
    scale = 128
    packed = jnp.concatenate(
        [
            z3_half,
            z2,
            (positives // scale).astype(jnp.bfloat16)[:, None],
            (positives % scale).astype(jnp.bfloat16)[:, None],
        ],
        axis=1,
    )
    gathered = gather_rows(packed)
    z3_all = gathered[:, :width]
    z2_all = gathered[:, width : 2 * width]
    pos_all = gathered[:, 2 * width].astype(jnp.int32) * scale + gathered[:, 2 * width + 1].astype(
        jnp.int32
    )
    batch_rows = z2_all.shape[0]
    logits = jnp.dot(z3_all, z2_all.T, preferred_element_type=jnp.float32)
    expo = jnp.exp(logits)
    row_lse = jnp.log(jnp.sum(expo, axis=1))
    col_lse = jnp.log(jnp.sum(expo, axis=0))
    columns = jnp.arange(batch_rows)
    is_positive = pos_all[:, None] == columns[None, :]
    positive_score = jnp.sum(jnp.where(is_positive, logits, 0.0), axis=1)
    loss = (jnp.sum(0.5 * row_lse - positive_score) + 0.5 * jnp.sum(col_lse)) / batch_rows
    slope = (
        0.5 * jnp.exp(logits - row_lse[:, None])
        + 0.5 * jnp.exp(logits - col_lse[None, :])
        - is_positive.astype(jnp.float32)
    ).astype(jnp.bfloat16)
    block = flat_index()
    first = block * own_rows
    grad_cols = lax.dot_general(
        slope, z3_all, (((0,), (0,)), ((), ())), preferred_element_type=jnp.float32
    )
    grad_z2 = lax.dynamic_slice_in_dim(grad_cols, first, own_rows, axis=0)
    grad_rows = jnp.dot(slope, z2_all, preferred_element_type=jnp.float32)
    grad_unit = lax.dynamic_slice_in_dim(grad_rows, first, own_rows, axis=0)
    grad_z3 = unit_backward(z3, inverse, grad_unit)
    pieces, bias_slope = pullback(grad_z3)
    grad_bias = bias_backward(distance, bias_slope, bias_weight.shape[0])
    big = jnp.concatenate([pieces[0], pieces[1]], axis=1)
    span = big.shape[1]
    small = jnp.concatenate(
        [
            pieces[2].reshape(-1),
            grad_bias.reshape(-1).astype(jnp.bfloat16),
            pieces[3].reshape(-1).astype(jnp.bfloat16),
        ]
    )
    small_size = small.shape[0]
    small_rows = -(-small_size // span)
    small = jnp.pad(small, (0, small_rows * span - small_size)).reshape(small_rows, span)
    count = device_count()
    rows = big.shape[0] + small_rows
    parts = 2
    padded = -(-rows // (count * parts)) * (count * parts)
    joined = jnp.concatenate(
        [big, small, jnp.zeros((padded - rows, span), jnp.bfloat16)], axis=0
    )
    (total,) = sum_rows((joined,), parts)
    qkv_cols = w_qkv.shape[1]
    weight_rows = w_qkv.shape[0]
    grad_qkv = total[:weight_rows, :qkv_cols]
    grad_out = total[:weight_rows, qkv_cols:]
    tail = total[weight_rows : weight_rows + small_rows].reshape(-1)
    proj_size = proj.size
    bias_size = bias_weight.size
    grad_proj = tail[:proj_size].reshape(proj.shape)
    grad_bias_all = tail[proj_size : proj_size + bias_size].reshape(bias_weight.shape)
    grad_gain = tail[proj_size + bias_size : proj_size + bias_size + ln_gain.size]
    return (loss, grad_z2, grad_qkv, grad_out, grad_proj, grad_bias_all, grad_gain)


def solution(mesh):
    return jax.shard_map(
        on_device,
        mesh=mesh,
        in_specs=(
            P(("dp", "group"), None, None),
            P(("dp", "group"), None, None),
            P(("dp", "group")),
            P(("dp", "group")),
            P(("dp", "group"), None),
            P(),
            P(),
            P(),
            P(),
            P(),
        ),
        out_specs=(P(), P(("dp", "group"), None), P(), P(), P(), P(), P()),
        check_vma=False,
    )
```

```python
import math

import jax
import jax.numpy as jnp
from jax import lax
from jax.sharding import PartitionSpec as P


def pair_distance(coords):
    offsets = coords[:, :, :, None] - coords[:, :, None, :]
    return jnp.sqrt(jnp.sum(offsets * offsets, axis=1) + 0.25)


def kernel_values(distance, kernels):
    centers = jnp.arange(kernels).astype(jnp.float32) * (12.0 / kernels)
    return jnp.exp(-(((distance[..., None] - centers) / 0.5) ** 2))


def group_split(values, width):
    return values.reshape((values.shape[0] // width, width) + values.shape[1:])


def bias_forward(distance, bias_weight):
    basis = kernel_values(distance, bias_weight.shape[0])
    return jnp.einsum("mijk,kh->mhij", basis, bias_weight, precision=lax.Precision.HIGH)


def bias_backward(distance, bias_slope, kernels):
    basis = kernel_values(distance, kernels)
    return jnp.einsum("mijk,mhij->kh", basis, bias_slope, precision=lax.Precision.HIGH)


def encode_core(params_in, pair_bias, feats, counts):
    w_qkv, w_out, proj, ln_gain = params_in
    mol_count, atom_count, model_width = feats.shape
    head_count = pair_bias.shape[1]
    head_dim = model_width // head_count
    inputs = feats.astype(jnp.float32)
    center = jnp.mean(inputs, axis=-1, keepdims=True)
    spread = jnp.mean((inputs - center) ** 2, axis=-1, keepdims=True)
    normed = ((inputs - center) * lax.rsqrt(spread + 1e-05) * ln_gain).astype(jnp.bfloat16)
    split_weight = w_qkv.reshape(model_width, 3, head_count, head_dim)
    projected = jnp.einsum(
        "mia,achd->cmhid", normed, split_weight, preferred_element_type=jnp.float32
    ).astype(jnp.bfloat16)
    query_heads = projected[0]
    key_heads = projected[1]
    value_heads = projected[2]
    scores = (
        jnp.einsum("mhid,mhjd->mhij", query_heads, key_heads, preferred_element_type=jnp.float32)
        * head_dim ** (-0.5)
        + pair_bias
    )
    is_valid = jnp.arange(atom_count)[None, :] < counts[:, None]
    scores = jnp.where(is_valid[:, None, None, :], scores, -1e30)
    highest = jnp.max(scores, axis=-1, keepdims=True)
    expo = jnp.exp(scores - highest)
    attn_weights = (expo / jnp.sum(expo, axis=-1, keepdims=True)).astype(jnp.bfloat16)
    context = jnp.einsum(
        "mhij,mhjd->mihd", attn_weights, value_heads, preferred_element_type=jnp.float32
    ).astype(jnp.bfloat16)
    hidden = inputs + jnp.dot(
        context.reshape(mol_count * atom_count, model_width),
        w_out,
        preferred_element_type=jnp.float32,
    ).reshape(mol_count, atom_count, model_width)
    pooled = jnp.sum(jnp.where(is_valid[..., None], hidden, 0.0), axis=1)
    return jnp.dot(pooled.astype(jnp.bfloat16), proj, preferred_element_type=jnp.float32)


def unit_rows(values):
    inverse = lax.rsqrt(jnp.mean(values * values, axis=1, keepdims=True) + 1e-06) * values.shape[
        1
    ] ** (-0.5)
    return (values * inverse, inverse)


def unit_backward(values, inverse, grad):
    along = jnp.sum(values * grad, axis=1, keepdims=True)
    return inverse * (grad - values * along * (inverse * inverse))


def flat_index():
    return lax.axis_index("dp") * lax.axis_size("group") + lax.axis_index("group")


def device_count():
    return lax.axis_size("dp") * lax.axis_size("group")


def step_bits(count, part=0, parts=1):
    steps = count.bit_length() - 1
    assert 1 << steps == count
    if steps < 2:
        return list(range(steps))
    outer = [0] + list(range(2, steps))
    turn = (part * len(outer)) // parts
    return [1] + outer[turn:] + outer[:turn]


def swap_with(value, bit, count):
    pairs = [(i, i ^ (1 << bit)) for i in range(count)]
    return lax.ppermute(value, ("dp", "group"), pairs)


def gather_rows(value):
    count = device_count()
    index = flat_index()
    current = value
    for bit in range(count.bit_length() - 1):
        other = swap_with(current, bit, count)
        low = (index >> bit) % 2 == 0
        current = jnp.where(
            low, jnp.concatenate([current, other]), jnp.concatenate([other, current])
        )
    return current


def sum_rows(values, parts=1):
    count = device_count()
    index = flat_index()
    orders = [step_bits(count, p, parts) for p in range(parts)]
    current = []
    for v in values:
        share = v.shape[0] // parts
        current += [v[p * share : (p + 1) * share].astype(jnp.float32) for p in range(parts)]
    order_of = [orders[i % parts] for i in range(len(current))]
    for step in range(len(orders[0])):
        sent_all, kept_all = [], []
        for v, order in zip(current, order_of):
            side = (index >> order[step]) % 2
            half = v.shape[0] // 2
            kept_all.append(lax.dynamic_slice_in_dim(v, side * half, half, axis=0))
            sent = lax.dynamic_slice_in_dim(v, (1 - side) * half, half, axis=0)
            sent_all.append(swap_with(sent.astype(jnp.bfloat16), order[step], count))
        current = [k + c.astype(jnp.float32) for k, c in zip(kept_all, sent_all)]
    current = [v.astype(jnp.bfloat16) for v in current]
    for step in reversed(range(len(orders[0]))):
        joined = []
        for v, order in zip(current, order_of):
            low = (index >> order[step]) % 2 == 0
            c = swap_with(v, order[step], count)
            joined.append(jnp.where(low, jnp.concatenate([v, c]), jnp.concatenate([c, v])))
        current = joined
    merged = []
    for i in range(len(values)):
        merged.append(jnp.concatenate(current[i * parts : (i + 1) * parts]).astype(jnp.float32))
    return merged


def on_device(
    atom_feats, coords, atom_counts, positives, z2, w_qkv, w_out, proj, bias_weight, ln_gain
):
    distance = pair_distance(coords)
    pair_bias = bias_forward(distance, bias_weight)

    def local_encode(params_in, bias_in):
        return encode_core(params_in, bias_in, atom_feats, atom_counts)

    z3, pullback = jax.vjp(local_encode, (w_qkv, w_out, proj, ln_gain), pair_bias)
    unit, inverse = unit_rows(z3)
    z3_half = unit.astype(jnp.bfloat16)
    own_rows = z3.shape[0]
    width = z3.shape[1]
    scale = 128
    packed = jnp.concatenate(
        [
            z3_half,
            z2,
            (positives // scale).astype(jnp.bfloat16)[:, None],
            (positives % scale).astype(jnp.bfloat16)[:, None],
        ],
        axis=1,
    )
    gathered = gather_rows(packed)
    z3_all = gathered[:, :width]
    z2_all = gathered[:, width : 2 * width]
    pos_all = gathered[:, 2 * width].astype(jnp.int32) * scale + gathered[:, 2 * width + 1].astype(
        jnp.int32
    )
    batch_rows = z2_all.shape[0]
    logits = jnp.dot(z3_all, z2_all.T, preferred_element_type=jnp.float32)
    expo = jnp.exp(logits)
    row_lse = jnp.log(jnp.sum(expo, axis=1))
    col_lse = jnp.log(jnp.sum(expo, axis=0))
    columns = jnp.arange(batch_rows)
    is_positive = pos_all[:, None] == columns[None, :]
    positive_score = jnp.sum(jnp.where(is_positive, logits, 0.0), axis=1)
    loss = (jnp.sum(0.5 * row_lse - positive_score) + 0.5 * jnp.sum(col_lse)) / batch_rows
    slope = (
        0.5 * jnp.exp(logits - row_lse[:, None])
        + 0.5 * jnp.exp(logits - col_lse[None, :])
        - is_positive.astype(jnp.float32)
    ).astype(jnp.bfloat16)
    block = flat_index()
    first = block * own_rows
    grad_cols = lax.dot_general(
        slope, z3_all, (((0,), (0,)), ((), ())), preferred_element_type=jnp.float32
    )
    grad_z2 = lax.dynamic_slice_in_dim(grad_cols, first, own_rows, axis=0)
    grad_rows = jnp.dot(slope, z2_all, preferred_element_type=jnp.float32)
    grad_unit = lax.dynamic_slice_in_dim(grad_rows, first, own_rows, axis=0)
    grad_z3 = unit_backward(z3, inverse, grad_unit)
    pieces, bias_slope = pullback(grad_z3)
    grad_bias = bias_backward(distance, bias_slope, bias_weight.shape[0])
    big = jnp.concatenate([pieces[0], pieces[1]], axis=1)
    span = big.shape[1]
    small = jnp.concatenate(
        [
            pieces[2].reshape(-1),
            grad_bias.reshape(-1).astype(jnp.bfloat16),
            pieces[3].reshape(-1).astype(jnp.bfloat16),
        ]
    )
    small_size = small.shape[0]
    small_rows = -(-small_size // span)
    small = jnp.pad(small, (0, small_rows * span - small_size)).reshape(small_rows, span)
    count = device_count()
    rows = big.shape[0] + small_rows
    parts = 2
    padded = -(-rows // (count * parts)) * (count * parts)
    joined = jnp.concatenate(
        [big, small, jnp.zeros((padded - rows, span), jnp.bfloat16)], axis=0
    )
    (total,) = sum_rows((joined,), parts)
    qkv_cols = w_qkv.shape[1]
    weight_rows = w_qkv.shape[0]
    grad_qkv = total[:weight_rows, :qkv_cols]
    grad_out = total[:weight_rows, qkv_cols:]
    tail = total[weight_rows : weight_rows + small_rows].reshape(-1)
    proj_size = proj.size
    bias_size = bias_weight.size
    grad_proj = tail[:proj_size].reshape(proj.shape)
    grad_bias_all = tail[proj_size : proj_size + bias_size].reshape(bias_weight.shape)
    grad_gain = tail[proj_size + bias_size : proj_size + bias_size + ln_gain.size]
    return (loss, grad_z2, grad_qkv, grad_out, grad_proj, grad_bias_all, grad_gain)


def solution(mesh):
    return jax.shard_map(
        on_device,
        mesh=mesh,
        in_specs=(
            P(("dp", "group"), None, None),
            P(("dp", "group"), None, None),
            P(("dp", "group")),
            P(("dp", "group")),
            P(("dp", "group"), None),
            P(),
            P(),
            P(),
            P(),
            P(),
        ),
        out_specs=(P(), P(("dp", "group"), None), P(), P(), P(), P(), P()),
        check_vma=False,
    )
```

```python
import math

import jax
import jax.numpy as jnp
from jax import lax
from jax.sharding import PartitionSpec as P


def pair_distance(coords):
    offsets = coords[:, :, :, None] - coords[:, :, None, :]
    return jnp.sqrt(jnp.sum(offsets * offsets, axis=1) + 0.25)


def kernel_values(distance, kernels):
    centers = jnp.arange(kernels).astype(jnp.float32) * (12.0 / kernels)
    return jnp.exp(-(((distance[..., None] - centers) / 0.5) ** 2))


def group_split(values, width):
    return values.reshape((values.shape[0] // width, width) + values.shape[1:])


def bias_forward(distance, bias_weight):
    basis = kernel_values(distance, bias_weight.shape[0])
    return jnp.einsum("mijk,kh->mhij", basis, bias_weight, precision=lax.Precision.HIGH)


def bias_backward(distance, bias_slope, kernels):
    basis = kernel_values(distance, kernels)
    return jnp.einsum("mijk,mhij->kh", basis, bias_slope, precision=lax.Precision.HIGH)


def encode_core(params_in, pair_bias, feats, counts):
    w_qkv, w_out, proj, ln_gain = params_in
    mol_count, atom_count, model_width = feats.shape
    head_count = pair_bias.shape[1]
    head_dim = model_width // head_count
    inputs = feats.astype(jnp.float32)
    center = jnp.mean(inputs, axis=-1, keepdims=True)
    spread = jnp.mean((inputs - center) ** 2, axis=-1, keepdims=True)
    normed = ((inputs - center) * lax.rsqrt(spread + 1e-05) * ln_gain).astype(jnp.bfloat16)
    split_weight = w_qkv.reshape(model_width, 3, head_count, head_dim)
    projected = jnp.einsum(
        "mia,achd->cmhid", normed, split_weight, preferred_element_type=jnp.float32
    ).astype(jnp.bfloat16)
    query_heads = projected[0]
    key_heads = projected[1]
    value_heads = projected[2]
    scores = (
        jnp.einsum("mhid,mhjd->mhij", query_heads, key_heads, preferred_element_type=jnp.float32)
        * head_dim ** (-0.5)
        + pair_bias
    )
    is_valid = jnp.arange(atom_count)[None, :] < counts[:, None]
    scores = jnp.where(is_valid[:, None, None, :], scores, -1e30)
    highest = jnp.max(scores, axis=-1, keepdims=True)
    expo = jnp.exp(scores - highest)
    attn_weights = (expo / jnp.sum(expo, axis=-1, keepdims=True)).astype(jnp.bfloat16)
    context = jnp.einsum(
        "mhij,mhjd->mhid", attn_weights, value_heads, preferred_element_type=jnp.float32
    ).astype(jnp.bfloat16)
    context_sum = jnp.sum(
        jnp.where(is_valid[:, None, :, None], context.astype(jnp.float32), 0.0), axis=2
    )
    input_sum = jnp.sum(jnp.where(is_valid[..., None], inputs, 0.0), axis=1)
    split_out = w_out.reshape(head_count, head_dim, model_width).astype(jnp.float32)
    pooled = input_sum + jnp.einsum(
        "mhd,hdo->mo", context_sum, split_out, precision=lax.Precision.HIGHEST
    )
    return jnp.dot(pooled.astype(jnp.bfloat16), proj, preferred_element_type=jnp.float32)


def unit_rows(values):
    inverse = lax.rsqrt(jnp.mean(values * values, axis=1, keepdims=True) + 1e-06) * values.shape[
        1
    ] ** (-0.5)
    return (values * inverse, inverse)


def unit_backward(values, inverse, grad):
    along = jnp.sum(values * grad, axis=1, keepdims=True)
    return inverse * (grad - values * along * (inverse * inverse))


def flat_index():
    return lax.axis_index("dp") * lax.axis_size("group") + lax.axis_index("group")


def device_count():
    return lax.axis_size("dp") * lax.axis_size("group")


def step_bits(count, part=0, parts=1):
    steps = count.bit_length() - 1
    assert 1 << steps == count
    if steps < 2:
        return list(range(steps))
    outer = [0] + list(range(2, steps))
    turn = (part * len(outer)) // parts
    return [1] + outer[turn:] + outer[:turn]


def swap_with(value, bit, count):
    pairs = [(i, i ^ (1 << bit)) for i in range(count)]
    return lax.ppermute(value, ("dp", "group"), pairs)


def gather_rows(value):
    count = device_count()
    index = flat_index()
    current = value
    for bit in range(count.bit_length() - 1):
        other = swap_with(current, bit, count)
        low = (index >> bit) % 2 == 0
        current = jnp.where(
            low, jnp.concatenate([current, other]), jnp.concatenate([other, current])
        )
    return current


def sum_rows(values, parts=1):
    count = device_count()
    index = flat_index()
    orders = [step_bits(count, p, parts) for p in range(parts)]
    current = []
    for v in values:
        share = v.shape[0] // parts
        current += [v[p * share : (p + 1) * share].astype(jnp.float32) for p in range(parts)]
    order_of = [orders[i % parts] for i in range(len(current))]
    for step in range(len(orders[0])):
        sent_all, kept_all = [], []
        for v, order in zip(current, order_of):
            side = (index >> order[step]) % 2
            half = v.shape[0] // 2
            kept_all.append(lax.dynamic_slice_in_dim(v, side * half, half, axis=0))
            sent = lax.dynamic_slice_in_dim(v, (1 - side) * half, half, axis=0)
            sent_all.append(swap_with(sent.astype(jnp.bfloat16), order[step], count))
        current = [k + c.astype(jnp.float32) for k, c in zip(kept_all, sent_all)]
    current = [v.astype(jnp.bfloat16) for v in current]
    for step in reversed(range(len(orders[0]))):
        joined = []
        for v, order in zip(current, order_of):
            low = (index >> order[step]) % 2 == 0
            c = swap_with(v, order[step], count)
            joined.append(jnp.where(low, jnp.concatenate([v, c]), jnp.concatenate([c, v])))
        current = joined
    merged = []
    for i in range(len(values)):
        merged.append(jnp.concatenate(current[i * parts : (i + 1) * parts]).astype(jnp.float32))
    return merged


def on_device(
    atom_feats, coords, atom_counts, positives, z2, w_qkv, w_out, proj, bias_weight, ln_gain
):
    distance = pair_distance(coords)
    pair_bias = bias_forward(distance, bias_weight)

    def local_encode(params_in, bias_in):
        return encode_core(params_in, bias_in, atom_feats, atom_counts)

    z3, pullback = jax.vjp(local_encode, (w_qkv, w_out, proj, ln_gain), pair_bias)
    unit, inverse = unit_rows(z3)
    z3_half = unit.astype(jnp.bfloat16)
    own_rows = z3.shape[0]
    width = z3.shape[1]
    scale = 128
    packed = jnp.concatenate(
        [
            z3_half,
            z2,
            (positives // scale).astype(jnp.bfloat16)[:, None],
            (positives % scale).astype(jnp.bfloat16)[:, None],
        ],
        axis=1,
    )
    gathered = gather_rows(packed)
    z3_all = gathered[:, :width]
    z2_all = gathered[:, width : 2 * width]
    pos_all = gathered[:, 2 * width].astype(jnp.int32) * scale + gathered[:, 2 * width + 1].astype(
        jnp.int32
    )
    batch_rows = z2_all.shape[0]
    logits = jnp.dot(z3_all, z2_all.T, preferred_element_type=jnp.float32)
    expo = jnp.exp(logits)
    row_lse = jnp.log(jnp.sum(expo, axis=1))
    col_lse = jnp.log(jnp.sum(expo, axis=0))
    columns = jnp.arange(batch_rows)
    is_positive = pos_all[:, None] == columns[None, :]
    positive_score = jnp.sum(jnp.where(is_positive, logits, 0.0), axis=1)
    loss = (jnp.sum(0.5 * row_lse - positive_score) + 0.5 * jnp.sum(col_lse)) / batch_rows
    slope = (
        0.5 * jnp.exp(logits - row_lse[:, None])
        + 0.5 * jnp.exp(logits - col_lse[None, :])
        - is_positive.astype(jnp.float32)
    ).astype(jnp.bfloat16)
    block = flat_index()
    first = block * own_rows
    grad_cols = lax.dot_general(
        slope, z3_all, (((0,), (0,)), ((), ())), preferred_element_type=jnp.float32
    )
    grad_z2 = lax.dynamic_slice_in_dim(grad_cols, first, own_rows, axis=0)
    grad_rows = jnp.dot(slope, z2_all, preferred_element_type=jnp.float32)
    grad_unit = lax.dynamic_slice_in_dim(grad_rows, first, own_rows, axis=0)
    grad_z3 = unit_backward(z3, inverse, grad_unit)
    pieces, bias_slope = pullback(grad_z3)
    grad_bias = bias_backward(distance, bias_slope, bias_weight.shape[0])
    big = jnp.concatenate([pieces[0], pieces[1]], axis=1)
    span = big.shape[1]
    small = jnp.concatenate(
        [
            pieces[2].reshape(-1),
            grad_bias.reshape(-1).astype(jnp.bfloat16),
            pieces[3].reshape(-1).astype(jnp.bfloat16),
        ]
    )
    small_size = small.shape[0]
    small_rows = -(-small_size // span)
    small = jnp.pad(small, (0, small_rows * span - small_size)).reshape(small_rows, span)
    count = device_count()
    rows = big.shape[0] + small_rows
    parts = 2
    padded = -(-rows // (count * parts)) * (count * parts)
    joined = jnp.concatenate(
        [big, small, jnp.zeros((padded - rows, span), jnp.bfloat16)], axis=0
    )
    (total,) = sum_rows((joined,), parts)
    qkv_cols = w_qkv.shape[1]
    weight_rows = w_qkv.shape[0]
    grad_qkv = total[:weight_rows, :qkv_cols]
    grad_out = total[:weight_rows, qkv_cols:]
    tail = total[weight_rows : weight_rows + small_rows].reshape(-1)
    proj_size = proj.size
    bias_size = bias_weight.size
    grad_proj = tail[:proj_size].reshape(proj.shape)
    grad_bias_all = tail[proj_size : proj_size + bias_size].reshape(bias_weight.shape)
    grad_gain = tail[proj_size + bias_size : proj_size + bias_size + ln_gain.size]
    return (loss, grad_z2, grad_qkv, grad_out, grad_proj, grad_bias_all, grad_gain)


def solution(mesh):
    return jax.shard_map(
        on_device,
        mesh=mesh,
        in_specs=(
            P(("dp", "group"), None, None),
            P(("dp", "group"), None, None),
            P(("dp", "group")),
            P(("dp", "group")),
            P(("dp", "group"), None),
            P(),
            P(),
            P(),
            P(),
            P(),
        ),
        out_specs=(P(), P(("dp", "group"), None), P(), P(), P(), P(), P()),
        check_vma=False,
    )
```

```python
import math

import jax
import jax.numpy as jnp
from jax import lax
from jax.sharding import PartitionSpec as P


def pair_distance(coords):
    offsets = coords[:, :, :, None] - coords[:, :, None, :]
    return jnp.sqrt(jnp.sum(offsets * offsets, axis=1) + 0.25)


def kernel_values(distance, kernels):
    centers = jnp.arange(kernels).astype(jnp.float32) * (12.0 / kernels)
    return jnp.exp(-(((distance[..., None] - centers) / 0.5) ** 2))


def group_split(values, width):
    return values.reshape((values.shape[0] // width, width) + values.shape[1:])


def bias_forward(distance, bias_weight):
    basis = kernel_values(distance, bias_weight.shape[0])
    return jnp.einsum("mijk,kh->mhij", basis, bias_weight, precision=lax.Precision.HIGH)


def bias_backward(distance, bias_slope, kernels):
    basis = kernel_values(distance, kernels)
    return jnp.einsum("mijk,mhij->kh", basis, bias_slope, precision=lax.Precision.HIGH)


def encode_core(params_in, pair_bias, feats, counts):
    w_qkv, w_out, proj, ln_gain = params_in
    mol_count, atom_count, model_width = feats.shape
    head_count = pair_bias.shape[1]
    head_dim = model_width // head_count
    inputs = feats.astype(jnp.float32)
    center = jnp.mean(inputs, axis=-1, keepdims=True)
    spread = jnp.mean((inputs - center) ** 2, axis=-1, keepdims=True)
    normed = ((inputs - center) * lax.rsqrt(spread + 1e-05) * ln_gain).astype(jnp.bfloat16)
    split_weight = w_qkv.reshape(model_width, 3, head_count, head_dim)
    projected = jnp.einsum(
        "mia,achd->cmhid", normed, split_weight, preferred_element_type=jnp.float32
    ).astype(jnp.bfloat16)
    query_heads = projected[0]
    key_heads = projected[1]
    value_heads = projected[2]
    scores = (
        jnp.einsum("mhid,mhjd->mhij", query_heads, key_heads, preferred_element_type=jnp.float32)
        * head_dim ** (-0.5)
        + pair_bias
    )
    is_valid = jnp.arange(atom_count)[None, :] < counts[:, None]
    scores = jnp.where(is_valid[:, None, None, :], scores, -1e30)
    highest = jnp.max(scores, axis=-1, keepdims=True)
    expo = jnp.exp(scores - highest)
    attn_weights = (expo / jnp.sum(expo, axis=-1, keepdims=True)).astype(jnp.bfloat16)
    context = jnp.einsum(
        "mhij,mhjd->mhid", attn_weights, value_heads, preferred_element_type=jnp.float32
    ).astype(jnp.bfloat16)
    context_sum = jnp.sum(
        jnp.where(is_valid[:, None, :, None], context.astype(jnp.float32), 0.0), axis=2
    )
    input_sum = jnp.sum(jnp.where(is_valid[..., None], inputs, 0.0), axis=1)
    split_out = w_out.reshape(head_count, head_dim, model_width).astype(jnp.float32)
    pooled = input_sum + jnp.einsum(
        "mhd,hdo->mo", context_sum, split_out, precision=lax.Precision.HIGHEST
    )
    return jnp.dot(pooled.astype(jnp.bfloat16), proj, preferred_element_type=jnp.float32)


def unit_rows(values):
    inverse = lax.rsqrt(jnp.mean(values * values, axis=1, keepdims=True) + 1e-06) * values.shape[
        1
    ] ** (-0.5)
    return (values * inverse, inverse)


def unit_backward(values, inverse, grad):
    along = jnp.sum(values * grad, axis=1, keepdims=True)
    return inverse * (grad - values * along * (inverse * inverse))


def flat_index():
    return lax.axis_index("dp") * lax.axis_size("group") + lax.axis_index("group")


def device_count():
    return lax.axis_size("dp") * lax.axis_size("group")


def step_bits(count, part=0, parts=1):
    steps = count.bit_length() - 1
    assert 1 << steps == count
    if steps < 2:
        return list(range(steps))
    outer = [0] + list(range(2, steps))
    turn = (part * len(outer)) // parts
    return [1] + outer[turn:] + outer[:turn]


def swap_with(value, bit, count):
    pairs = [(i, i ^ (1 << bit)) for i in range(count)]
    return lax.ppermute(value, ("dp", "group"), pairs)


def gather_rows(value):
    count = device_count()
    index = flat_index()
    current = value
    for bit in range(count.bit_length() - 1):
        other = swap_with(current, bit, count)
        low = (index >> bit) % 2 == 0
        current = jnp.where(
            low, jnp.concatenate([current, other]), jnp.concatenate([other, current])
        )
    return current


def sum_rows(values, parts=1):
    count = device_count()
    index = flat_index()
    orders = [step_bits(count, p, parts) for p in range(parts)]
    current = []
    for v in values:
        share = v.shape[0] // parts
        current += [v[p * share : (p + 1) * share].astype(jnp.float32) for p in range(parts)]
    order_of = [orders[i % parts] for i in range(len(current))]
    for step in range(len(orders[0])):
        sent_all, kept_all = [], []
        for v, order in zip(current, order_of):
            side = (index >> order[step]) % 2
            half = v.shape[0] // 2
            kept_all.append(lax.dynamic_slice_in_dim(v, side * half, half, axis=0))
            sent = lax.dynamic_slice_in_dim(v, (1 - side) * half, half, axis=0)
            sent_all.append(swap_with(sent.astype(jnp.bfloat16), order[step], count))
        current = [k + c.astype(jnp.float32) for k, c in zip(kept_all, sent_all)]
    current = [v.astype(jnp.bfloat16) for v in current]
    for step in reversed(range(len(orders[0]))):
        joined = []
        for v, order in zip(current, order_of):
            low = (index >> order[step]) % 2 == 0
            c = swap_with(v, order[step], count)
            joined.append(jnp.where(low, jnp.concatenate([v, c]), jnp.concatenate([c, v])))
        current = joined
    merged = []
    for i in range(len(values)):
        merged.append(jnp.concatenate(current[i * parts : (i + 1) * parts]).astype(jnp.float32))
    return merged


def on_device(
    atom_feats, coords, atom_counts, positives, z2, w_qkv, w_out, proj, bias_weight, ln_gain
):
    distance = pair_distance(coords)
    pair_bias = bias_forward(distance, bias_weight)

    def local_encode(params_in, bias_in):
        return encode_core(params_in, bias_in, atom_feats, atom_counts)

    z3, pullback = jax.vjp(local_encode, (w_qkv, w_out, proj, ln_gain), pair_bias)
    unit, inverse = unit_rows(z3)
    z3_half = unit.astype(jnp.bfloat16)
    own_rows = z3.shape[0]
    width = z3.shape[1]
    scale = 128
    packed = jnp.concatenate(
        [
            z3_half,
            z2,
            (positives // scale).astype(jnp.bfloat16)[:, None],
            (positives % scale).astype(jnp.bfloat16)[:, None],
        ],
        axis=1,
    )
    gathered = gather_rows(packed)
    z3_all = gathered[:, :width]
    z2_all = gathered[:, width : 2 * width]
    pos_all = gathered[:, 2 * width].astype(jnp.int32) * scale + gathered[:, 2 * width + 1].astype(
        jnp.int32
    )
    batch_rows = z2_all.shape[0]
    logits = jnp.dot(z3_all, z2_all.T, preferred_element_type=jnp.float32)
    expo = jnp.exp(logits)
    row_lse = jnp.log(jnp.sum(expo, axis=1))
    col_lse = jnp.log(jnp.sum(expo, axis=0))
    columns = jnp.arange(batch_rows)
    is_positive = pos_all[:, None] == columns[None, :]
    positive_score = jnp.sum(jnp.where(is_positive, logits, 0.0), axis=1)
    loss = (jnp.sum(0.5 * row_lse - positive_score) + 0.5 * jnp.sum(col_lse)) / batch_rows
    slope = (
        0.5 * jnp.exp(logits - row_lse[:, None])
        + 0.5 * jnp.exp(logits - col_lse[None, :])
        - is_positive.astype(jnp.float32)
    ).astype(jnp.bfloat16)
    block = flat_index()
    first = block * own_rows
    grad_cols = lax.dot_general(
        slope, z3_all, (((0,), (0,)), ((), ())), preferred_element_type=jnp.float32
    )
    grad_z2 = lax.dynamic_slice_in_dim(grad_cols, first, own_rows, axis=0)
    grad_rows = jnp.dot(slope, z2_all, preferred_element_type=jnp.float32)
    grad_unit = lax.dynamic_slice_in_dim(grad_rows, first, own_rows, axis=0)
    grad_z3 = unit_backward(z3, inverse, grad_unit)
    pieces, bias_slope = pullback(grad_z3)
    grad_bias = bias_backward(distance, bias_slope, bias_weight.shape[0])
    big = jnp.concatenate([pieces[0], pieces[1]], axis=1)
    span = big.shape[1]
    small = jnp.concatenate(
        [
            pieces[2].reshape(-1),
            grad_bias.reshape(-1).astype(jnp.bfloat16),
            pieces[3].reshape(-1).astype(jnp.bfloat16),
        ]
    )
    small_size = small.shape[0]
    small_rows = -(-small_size // span)
    small = jnp.pad(small, (0, small_rows * span - small_size)).reshape(small_rows, span)
    count = device_count()
    rows = big.shape[0] + small_rows
    parts = 3
    padded = -(-rows // (count * parts)) * (count * parts)
    joined = jnp.concatenate(
        [big, small, jnp.zeros((padded - rows, span), jnp.bfloat16)], axis=0
    )
    (total,) = sum_rows((joined,), parts)
    qkv_cols = w_qkv.shape[1]
    weight_rows = w_qkv.shape[0]
    grad_qkv = total[:weight_rows, :qkv_cols]
    grad_out = total[:weight_rows, qkv_cols:]
    tail = total[weight_rows : weight_rows + small_rows].reshape(-1)
    proj_size = proj.size
    bias_size = bias_weight.size
    grad_proj = tail[:proj_size].reshape(proj.shape)
    grad_bias_all = tail[proj_size : proj_size + bias_size].reshape(bias_weight.shape)
    grad_gain = tail[proj_size + bias_size : proj_size + bias_size + ln_gain.size]
    return (loss, grad_z2, grad_qkv, grad_out, grad_proj, grad_bias_all, grad_gain)


def solution(mesh):
    return jax.shard_map(
        on_device,
        mesh=mesh,
        in_specs=(
            P(("dp", "group"), None, None),
            P(("dp", "group"), None, None),
            P(("dp", "group")),
            P(("dp", "group")),
            P(("dp", "group"), None),
            P(),
            P(),
            P(),
            P(),
            P(),
        ),
        out_specs=(P(), P(("dp", "group"), None), P(), P(), P(), P(), P()),
        check_vma=False,
    )
```

```python
import math

import jax
import jax.numpy as jnp
from jax import lax
from jax.sharding import PartitionSpec as P


def pair_distance(coords):
    offsets = coords[:, :, :, None] - coords[:, :, None, :]
    return jnp.sqrt(jnp.sum(offsets * offsets, axis=1) + 0.25)


def kernel_values(distance, kernels):
    centers = jnp.arange(kernels).astype(jnp.float32) * (12.0 / kernels)
    return jnp.exp(-(((distance[..., None] - centers) / 0.5) ** 2))


def group_split(values, width):
    return values.reshape((values.shape[0] // width, width) + values.shape[1:])


def bias_forward(distance, bias_weight):
    basis = kernel_values(distance, bias_weight.shape[0])
    return jnp.einsum("mijk,kh->mhij", basis, bias_weight, precision=lax.Precision.HIGH)


def bias_backward(distance, bias_slope, kernels):
    basis = kernel_values(distance, kernels)
    return jnp.einsum("mijk,mhij->kh", basis, bias_slope, precision=lax.Precision.HIGH)


def encode_core(params_in, pair_bias, feats, counts):
    w_qkv, w_out, proj, ln_gain = params_in
    mol_count, atom_count, model_width = feats.shape
    head_count = pair_bias.shape[1]
    head_dim = model_width // head_count
    inputs = feats.astype(jnp.float32)
    center = jnp.mean(inputs, axis=-1, keepdims=True)
    spread = jnp.mean((inputs - center) ** 2, axis=-1, keepdims=True)
    normed = ((inputs - center) * lax.rsqrt(spread + 1e-05) * ln_gain).astype(jnp.bfloat16)
    split_weight = w_qkv.reshape(model_width, 3, head_count, head_dim)
    projected = jnp.einsum(
        "mia,achd->cmhid", normed, split_weight, preferred_element_type=jnp.float32
    ).astype(jnp.bfloat16)
    query_heads = projected[0]
    key_heads = projected[1]
    value_heads = projected[2]
    scores = (
        jnp.einsum("mhid,mhjd->mhij", query_heads, key_heads, preferred_element_type=jnp.float32)
        * head_dim ** (-0.5)
        + pair_bias
    )
    is_valid = jnp.arange(atom_count)[None, :] < counts[:, None]
    scores = jnp.where(is_valid[:, None, None, :], scores, -1e30)
    highest = jnp.max(scores, axis=-1, keepdims=True)
    expo = jnp.exp(scores - highest)
    attn_weights = (expo / jnp.sum(expo, axis=-1, keepdims=True)).astype(jnp.bfloat16)
    context = jnp.einsum(
        "mhij,mhjd->mhid", attn_weights, value_heads, preferred_element_type=jnp.float32
    ).astype(jnp.bfloat16)
    context_sum = jnp.sum(
        jnp.where(is_valid[:, None, :, None], context.astype(jnp.float32), 0.0), axis=2
    )
    input_sum = jnp.sum(jnp.where(is_valid[..., None], inputs, 0.0), axis=1)
    split_out = w_out.reshape(head_count, head_dim, model_width).astype(jnp.float32)
    pooled = input_sum + jnp.einsum(
        "mhd,hdo->mo", context_sum, split_out, precision=lax.Precision.HIGH
    )
    return jnp.dot(pooled.astype(jnp.bfloat16), proj, preferred_element_type=jnp.float32)


def unit_rows(values):
    inverse = lax.rsqrt(jnp.mean(values * values, axis=1, keepdims=True) + 1e-06) * values.shape[
        1
    ] ** (-0.5)
    return (values * inverse, inverse)


def unit_backward(values, inverse, grad):
    along = jnp.sum(values * grad, axis=1, keepdims=True)
    return inverse * (grad - values * along * (inverse * inverse))


def flat_index():
    return lax.axis_index("dp") * lax.axis_size("group") + lax.axis_index("group")


def device_count():
    return lax.axis_size("dp") * lax.axis_size("group")


def step_bits(count, part=0, parts=1):
    steps = count.bit_length() - 1
    assert 1 << steps == count
    if steps < 2:
        return list(range(steps))
    outer = [0] + list(range(2, steps))
    turn = (part * len(outer)) // parts
    return [1] + outer[turn:] + outer[:turn]


def swap_with(value, bit, count):
    pairs = [(i, i ^ (1 << bit)) for i in range(count)]
    return lax.ppermute(value, ("dp", "group"), pairs)


def gather_rows(value):
    count = device_count()
    index = flat_index()
    current = value
    for bit in range(count.bit_length() - 1):
        other = swap_with(current, bit, count)
        low = (index >> bit) % 2 == 0
        current = jnp.where(
            low, jnp.concatenate([current, other]), jnp.concatenate([other, current])
        )
    return current


def sum_rows(values, parts=1):
    count = device_count()
    index = flat_index()
    orders = [step_bits(count, p, parts) for p in range(parts)]
    current = []
    for v in values:
        share = v.shape[0] // parts
        current += [v[p * share : (p + 1) * share].astype(jnp.float32) for p in range(parts)]
    order_of = [orders[i % parts] for i in range(len(current))]
    for step in range(len(orders[0])):
        sent_all, kept_all = [], []
        for v, order in zip(current, order_of):
            side = (index >> order[step]) % 2
            half = v.shape[0] // 2
            kept_all.append(lax.dynamic_slice_in_dim(v, side * half, half, axis=0))
            sent = lax.dynamic_slice_in_dim(v, (1 - side) * half, half, axis=0)
            sent_all.append(swap_with(sent.astype(jnp.bfloat16), order[step], count))
        current = [k + c.astype(jnp.float32) for k, c in zip(kept_all, sent_all)]
    current = [v.astype(jnp.bfloat16) for v in current]
    for step in reversed(range(len(orders[0]))):
        joined = []
        for v, order in zip(current, order_of):
            low = (index >> order[step]) % 2 == 0
            c = swap_with(v, order[step], count)
            joined.append(jnp.where(low, jnp.concatenate([v, c]), jnp.concatenate([c, v])))
        current = joined
    merged = []
    for i in range(len(values)):
        merged.append(jnp.concatenate(current[i * parts : (i + 1) * parts]).astype(jnp.float32))
    return merged


def on_device(
    atom_feats, coords, atom_counts, positives, z2, w_qkv, w_out, proj, bias_weight, ln_gain
):
    distance = pair_distance(coords)
    pair_bias = bias_forward(distance, bias_weight)

    def local_encode(params_in, bias_in):
        return encode_core(params_in, bias_in, atom_feats, atom_counts)

    z3, pullback = jax.vjp(local_encode, (w_qkv, w_out, proj, ln_gain), pair_bias)
    unit, inverse = unit_rows(z3)
    z3_half = unit.astype(jnp.bfloat16)
    own_rows = z3.shape[0]
    width = z3.shape[1]
    scale = 128
    early = jnp.concatenate(
        [
            z2,
            (positives // scale).astype(jnp.bfloat16)[:, None],
            (positives % scale).astype(jnp.bfloat16)[:, None],
        ],
        axis=1,
    )
    early_all = gather_rows(early)
    z3_all = gather_rows(z3_half)
    z2_all = early_all[:, :width]
    pos_all = early_all[:, width].astype(jnp.int32) * scale + early_all[:, width + 1].astype(
        jnp.int32
    )
    batch_rows = z2_all.shape[0]
    logits = jnp.dot(z3_all, z2_all.T, preferred_element_type=jnp.float32)
    expo = jnp.exp(logits)
    row_lse = jnp.log(jnp.sum(expo, axis=1))
    col_lse = jnp.log(jnp.sum(expo, axis=0))
    columns = jnp.arange(batch_rows)
    is_positive = pos_all[:, None] == columns[None, :]
    positive_score = jnp.sum(jnp.where(is_positive, logits, 0.0), axis=1)
    loss = (jnp.sum(0.5 * row_lse - positive_score) + 0.5 * jnp.sum(col_lse)) / batch_rows
    slope = (
        0.5 * jnp.exp(logits - row_lse[:, None])
        + 0.5 * jnp.exp(logits - col_lse[None, :])
        - is_positive.astype(jnp.float32)
    ).astype(jnp.bfloat16)
    block = flat_index()
    first = block * own_rows
    grad_cols = lax.dot_general(
        slope, z3_all, (((0,), (0,)), ((), ())), preferred_element_type=jnp.float32
    )
    grad_z2 = lax.dynamic_slice_in_dim(grad_cols, first, own_rows, axis=0)
    grad_rows = jnp.dot(slope, z2_all, preferred_element_type=jnp.float32)
    grad_unit = lax.dynamic_slice_in_dim(grad_rows, first, own_rows, axis=0)
    grad_z3 = unit_backward(z3, inverse, grad_unit)
    pieces, bias_slope = pullback(grad_z3)
    grad_bias = bias_backward(distance, bias_slope, bias_weight.shape[0])
    big = jnp.concatenate([pieces[0], pieces[1]], axis=1)
    span = big.shape[1]
    small = jnp.concatenate(
        [
            pieces[2].reshape(-1),
            grad_bias.reshape(-1).astype(jnp.bfloat16),
            pieces[3].reshape(-1).astype(jnp.bfloat16),
        ]
    )
    small_size = small.shape[0]
    small_rows = -(-small_size // span)
    small = jnp.pad(small, (0, small_rows * span - small_size)).reshape(small_rows, span)
    count = device_count()
    rows = big.shape[0] + small_rows
    parts = 3
    padded = -(-rows // (count * parts)) * (count * parts)
    joined = jnp.concatenate(
        [big, small, jnp.zeros((padded - rows, span), jnp.bfloat16)], axis=0
    )
    (total,) = sum_rows((joined,), parts)
    qkv_cols = w_qkv.shape[1]
    weight_rows = w_qkv.shape[0]
    grad_qkv = total[:weight_rows, :qkv_cols]
    grad_out = total[:weight_rows, qkv_cols:]
    tail = total[weight_rows : weight_rows + small_rows].reshape(-1)
    proj_size = proj.size
    bias_size = bias_weight.size
    grad_proj = tail[:proj_size].reshape(proj.shape)
    grad_bias_all = tail[proj_size : proj_size + bias_size].reshape(bias_weight.shape)
    grad_gain = tail[proj_size + bias_size : proj_size + bias_size + ln_gain.size]
    return (loss, grad_z2, grad_qkv, grad_out, grad_proj, grad_bias_all, grad_gain)


def solution(mesh):
    return jax.shard_map(
        on_device,
        mesh=mesh,
        in_specs=(
            P(("dp", "group"), None, None),
            P(("dp", "group"), None, None),
            P(("dp", "group")),
            P(("dp", "group")),
            P(("dp", "group"), None),
            P(),
            P(),
            P(),
            P(),
            P(),
        ),
        out_specs=(P(), P(("dp", "group"), None), P(), P(), P(), P(), P()),
        check_vma=False,
    )
```

```python
import math

import jax
import jax.numpy as jnp
from jax import lax
from jax.sharding import PartitionSpec as P


def pair_distance(coords):
    offsets = coords[:, :, :, None] - coords[:, :, None, :]
    return jnp.sqrt(jnp.sum(offsets * offsets, axis=1) + 0.25)


def kernel_values(distance, kernels):
    centers = jnp.arange(kernels).astype(jnp.float32) * (12.0 / kernels)
    return jnp.exp(-(((distance[..., None] - centers) / 0.5) ** 2))


def group_split(values, width):
    return values.reshape((values.shape[0] // width, width) + values.shape[1:])


def bias_forward(distance, bias_weight):
    basis = kernel_values(distance, bias_weight.shape[0])
    return jnp.einsum("mijk,kh->mhij", basis, bias_weight, precision=lax.Precision.HIGH)


def bias_backward(distance, bias_slope, kernels):
    basis = kernel_values(distance, kernels)
    return jnp.einsum("mijk,mhij->kh", basis, bias_slope, precision=lax.Precision.HIGH)


def encode_core(params_in, pair_bias, feats, counts):
    w_qkv, w_out, proj, ln_gain = params_in
    mol_count, atom_count, model_width = feats.shape
    head_count = pair_bias.shape[1]
    head_dim = model_width // head_count
    inputs = feats.astype(jnp.float32)
    center = jnp.mean(inputs, axis=-1, keepdims=True)
    spread = jnp.mean((inputs - center) ** 2, axis=-1, keepdims=True)
    normed = ((inputs - center) * lax.rsqrt(spread + 1e-05) * ln_gain).astype(jnp.bfloat16)
    split_weight = w_qkv.reshape(model_width, 3, head_count, head_dim)
    projected = jnp.einsum(
        "mia,achd->cmhid", normed, split_weight, preferred_element_type=jnp.float32
    ).astype(jnp.bfloat16)
    query_heads = projected[0]
    key_heads = projected[1]
    value_heads = projected[2]
    scores = (
        jnp.einsum("mhid,mhjd->mhij", query_heads, key_heads, preferred_element_type=jnp.float32)
        * head_dim ** (-0.5)
        + pair_bias
    )
    is_valid = jnp.arange(atom_count)[None, :] < counts[:, None]
    scores = jnp.where(is_valid[:, None, None, :], scores, -1e30)
    highest = jnp.max(scores, axis=-1, keepdims=True)
    expo = jnp.exp(scores - highest)
    attn_weights = (expo / jnp.sum(expo, axis=-1, keepdims=True)).astype(jnp.bfloat16)
    context = jnp.einsum(
        "mhij,mhjd->mhid", attn_weights, value_heads, preferred_element_type=jnp.float32
    ).astype(jnp.bfloat16)
    context_sum = jnp.sum(
        jnp.where(is_valid[:, None, :, None], context.astype(jnp.float32), 0.0), axis=2
    )
    input_sum = jnp.sum(jnp.where(is_valid[..., None], inputs, 0.0), axis=1)
    split_out = w_out.reshape(head_count, head_dim, model_width).astype(jnp.float32)
    pooled = input_sum + jnp.einsum(
        "mhd,hdo->mo", context_sum, split_out, precision=lax.Precision.HIGH
    )
    return jnp.dot(pooled.astype(jnp.bfloat16), proj, preferred_element_type=jnp.float32)


def unit_rows(values):
    inverse = lax.rsqrt(jnp.mean(values * values, axis=1, keepdims=True) + 1e-06) * values.shape[
        1
    ] ** (-0.5)
    return (values * inverse, inverse)


def unit_backward(values, inverse, grad):
    along = jnp.sum(values * grad, axis=1, keepdims=True)
    return inverse * (grad - values * along * (inverse * inverse))


def flat_index():
    return lax.axis_index("dp") * lax.axis_size("group") + lax.axis_index("group")


def device_count():
    return lax.axis_size("dp") * lax.axis_size("group")


def step_bits(count, part=0, parts=1):
    steps = count.bit_length() - 1
    assert 1 << steps == count
    if steps < 2:
        return list(range(steps))
    outer = [0] + list(range(2, steps))
    turn = (part * len(outer)) // parts
    return [1] + outer[turn:] + outer[:turn]


def swap_with(value, bit, count):
    pairs = [(i, i ^ (1 << bit)) for i in range(count)]
    return lax.ppermute(value, ("dp", "group"), pairs)


def gather_rows(value):
    count = device_count()
    index = flat_index()
    current = value
    for bit in range(count.bit_length() - 1):
        other = swap_with(current, bit, count)
        low = (index >> bit) % 2 == 0
        current = jnp.where(
            low, jnp.concatenate([current, other]), jnp.concatenate([other, current])
        )
    return current


def sum_rows(values, parts=1, wire=jnp.bfloat16, tail=1):
    count = device_count()
    index = flat_index()
    orders = [step_bits(count, p, parts) for p in range(parts)]
    steps = len(orders[0])
    tail = min(tail, steps)
    split = steps - tail
    current = []
    for v in values:
        share = v.shape[0] // parts
        current += [v[p * share : (p + 1) * share].astype(jnp.float32) for p in range(parts)]
    order_of = [orders[i % parts] for i in range(len(current))]
    for step in range(split):
        sent_all, kept_all = [], []
        for v, order in zip(current, order_of):
            side = (index >> order[step]) % 2
            half = v.shape[0] // 2
            kept_all.append(lax.dynamic_slice_in_dim(v, side * half, half, axis=0))
            sent = lax.dynamic_slice_in_dim(v, (1 - side) * half, half, axis=0)
            sent_all.append(swap_with(sent.astype(wire), order[step], count))
        current = [k + c.astype(jnp.float32) for k, c in zip(kept_all, sent_all)]
    for step in range(split, steps):
        rounded = [v.astype(wire) for v in current]
        came = [swap_with(r, order[step], count) for r, order in zip(rounded, order_of)]
        current = [r.astype(jnp.float32) + c.astype(jnp.float32) for r, c in zip(rounded, came)]
    current = [v.astype(wire) for v in current]
    for step in reversed(range(split)):
        joined = []
        for v, order in zip(current, order_of):
            low = (index >> order[step]) % 2 == 0
            c = swap_with(v, order[step], count)
            joined.append(jnp.where(low, jnp.concatenate([v, c]), jnp.concatenate([c, v])))
        current = joined
    merged = []
    for i in range(len(values)):
        merged.append(jnp.concatenate(current[i * parts : (i + 1) * parts]).astype(jnp.float32))
    return merged


def on_device(
    atom_feats, coords, atom_counts, positives, z2, w_qkv, w_out, proj, bias_weight, ln_gain
):
    distance = pair_distance(coords)
    pair_bias = bias_forward(distance, bias_weight)

    def local_encode(params_in, bias_in):
        return encode_core(params_in, bias_in, atom_feats, atom_counts)

    z3, pullback = jax.vjp(local_encode, (w_qkv, w_out, proj, ln_gain), pair_bias)
    unit, inverse = unit_rows(z3)
    z3_half = unit.astype(jnp.bfloat16)
    own_rows = z3.shape[0]
    width = z3.shape[1]
    scale = 128
    early = jnp.concatenate(
        [
            z2,
            (positives // scale).astype(jnp.bfloat16)[:, None],
            (positives % scale).astype(jnp.bfloat16)[:, None],
        ],
        axis=1,
    )
    early_all = gather_rows(early)
    z3_all = gather_rows(z3_half)
    z2_all = early_all[:, :width]
    pos_all = early_all[:, width].astype(jnp.int32) * scale + early_all[:, width + 1].astype(
        jnp.int32
    )
    batch_rows = z2_all.shape[0]
    logits = jnp.dot(z3_all, z2_all.T, preferred_element_type=jnp.float32)
    expo = jnp.exp(logits)
    row_lse = jnp.log(jnp.sum(expo, axis=1))
    col_lse = jnp.log(jnp.sum(expo, axis=0))
    columns = jnp.arange(batch_rows)
    is_positive = pos_all[:, None] == columns[None, :]
    positive_score = jnp.sum(jnp.where(is_positive, logits, 0.0), axis=1)
    loss = (jnp.sum(0.5 * row_lse - positive_score) + 0.5 * jnp.sum(col_lse)) / batch_rows
    slope = (
        0.5 * jnp.exp(logits - row_lse[:, None])
        + 0.5 * jnp.exp(logits - col_lse[None, :])
        - is_positive.astype(jnp.float32)
    ).astype(jnp.bfloat16)
    block = flat_index()
    first = block * own_rows
    grad_cols = lax.dot_general(
        slope, z3_all, (((0,), (0,)), ((), ())), preferred_element_type=jnp.float32
    )
    grad_z2 = lax.dynamic_slice_in_dim(grad_cols, first, own_rows, axis=0)
    grad_rows = jnp.dot(slope, z2_all, preferred_element_type=jnp.float32)
    grad_unit = lax.dynamic_slice_in_dim(grad_rows, first, own_rows, axis=0)
    grad_z3 = unit_backward(z3, inverse, grad_unit)
    pieces, bias_slope = pullback(grad_z3)
    grad_bias = bias_backward(distance, bias_slope, bias_weight.shape[0])
    big = jnp.concatenate([pieces[0], pieces[1]], axis=1)
    span = big.shape[1]
    small = jnp.concatenate(
        [
            pieces[2].reshape(-1),
            grad_bias.reshape(-1).astype(jnp.bfloat16),
            pieces[3].reshape(-1).astype(jnp.bfloat16),
        ]
    )
    small_size = small.shape[0]
    small_rows = -(-small_size // span)
    small = jnp.pad(small, (0, small_rows * span - small_size)).reshape(small_rows, span)
    count = device_count()
    rows = big.shape[0] + small_rows
    parts = 3
    padded = -(-rows // (count * parts)) * (count * parts)
    joined = jnp.concatenate(
        [big, small, jnp.zeros((padded - rows, span), jnp.bfloat16)], axis=0
    )
    (total,) = sum_rows((joined,), parts)
    qkv_cols = w_qkv.shape[1]
    weight_rows = w_qkv.shape[0]
    grad_qkv = total[:weight_rows, :qkv_cols]
    grad_out = total[:weight_rows, qkv_cols:]
    tail = total[weight_rows : weight_rows + small_rows].reshape(-1)
    proj_size = proj.size
    bias_size = bias_weight.size
    grad_proj = tail[:proj_size].reshape(proj.shape)
    grad_bias_all = tail[proj_size : proj_size + bias_size].reshape(bias_weight.shape)
    grad_gain = tail[proj_size + bias_size : proj_size + bias_size + ln_gain.size]
    return (loss, grad_z2, grad_qkv, grad_out, grad_proj, grad_bias_all, grad_gain)


def solution(mesh):
    return jax.shard_map(
        on_device,
        mesh=mesh,
        in_specs=(
            P(("dp", "group"), None, None),
            P(("dp", "group"), None, None),
            P(("dp", "group")),
            P(("dp", "group")),
            P(("dp", "group"), None),
            P(),
            P(),
            P(),
            P(),
            P(),
        ),
        out_specs=(P(), P(("dp", "group"), None), P(), P(), P(), P(), P()),
        check_vma=False,
    )
```
